128 devices in a mesh: lon: 16 (over x_hi, y, core), lat: 8 (over x_lo, z).
Axes of the slice: x: 4 (x_hi: 2, x_lo: 2; x = x_hi * 2 + x_lo), y: 4, z: 4, core: 2. Of those that a mesh axis runs over, the one named last changes fastest.
Arguments:
- state: float32 [32, 128, 2048], P(None, 'lat', 'lon'), may hold values from -6 to 6
- land_mask: int32 [128, 2048], P('lat', 'lon'), may hold values 0 or 1
- observations: float32 [32, 131072], P(None, ('lon', 'lat')), may hold values from -6 to 6
- profile_cells: int32 [131072], P(('lon', 'lat')), may hold values from 0 to 2047
- profile_counts: int32 [128, 128], P(('lon', 'lat')), may hold values from 1 to 32, 1024 in all within a row
- w_in: bfloat16 [64, 32, 5, 5], replicated, may hold values from -0.21875 to 0.21875
- w_out: bfloat16 [32, 64, 5, 5], replicated, may hold values from -0.15625 to 0.15625
Outputs:
- final_state: float32 [32, 128, 2048], P(None, 'lat', 'lon')
- misfit: float32 [], replicated
- grad_in: float32 [64, 32, 5, 5], replicated
- grad_out: float32 [32, 64, 5, 5], replicated
- adjoint_state: float32 [32, 128, 2048], P(None, 'lat', 'lon')
The draws below stay inside these ranges and needn't reach their ends.
Inputs may be any that keep to these rules, and one draw needn't show every extreme that they name: `profile_counts`: each row sums to 1024, and in every row some entry equals 32.
All inputs are finite; a program needn't handle non-finite values. No bound on the sum of `land_mask` on one device may be relied on, other than what follows from the above.
Results may differ from the reference program's by a relative error of at most 0.0046.
Values may be sent and summed in bfloat16 or wider, within the bound.
No kernel may reach another device: no remote copies, remote signals or barrier semaphores. Data moves between devices by JAX's collectives and lax.ppermute only.
A program may use at most 64 MiB of HBM per device.

```python
import math
import jax
import jax.numpy as jnp
import numpy as np
from jax import lax

LEV = 32
HID = 64
KS = 5
STEPS = 2
CY = 16
CX = 128
CAP = 32
PROF_DEV = 1024
PROFILES = 131072
NY = 128
NX = 2048
N_LAT = 8
DEVICES = 128


def place_ends(drawn, rng, least, high):
    spot = [jax.random.randint(jax.random.fold_in(rng, axis), (), 0, length) for axis, length in enumerate(drawn.shape)]
    widest = drawn.shape.index(max(drawn.shape))
    next_to = spot[:widest] + [(spot[widest] + 1) % drawn.shape[widest]] + spot[widest + 1:]
    return drawn.at[tuple(spot)].set(least).at[tuple(next_to)].set(high)


def shard_levels(key, extent, cuts, low, largest):
    loudness, own = 1.0, jax.random.fold_in(key, 6)
    for position, parts in cuts:
        steps = jnp.exp(jax.random.uniform(jax.random.fold_in(own, position), (parts,), jnp.float32, low / len(cuts), largest / len(cuts)))
        loudness = loudness * jnp.repeat(steps, extent[position] // parts).reshape([-1 if axis == position else 1 for axis in range(len(extent))])
    return loudness


def length_profile(number_of, total, limit, skew):
    loads = [(1 << 20) // math.isqrt(grade ** skew) + 1 for grade in range(2, number_of + 1)]
    rest, counts = total - limit - (number_of - 1), [1] * (number_of - 1)
    while rest > 0:
        free = [i for i in range(number_of - 1) if counts[i] < limit]
        pool, budget = sum([loads[i] for i in free]), rest
        for i in free:
            addition = min(limit - counts[i], max(1, budget * loads[i] // pool), rest)
            counts[i] = counts[i] + addition
            rest = rest - addition
    return np.array([limit] + counts)


def uneven(rng, count, total, bound, lean):
    if count == 2:
        one = jax.random.randint(rng, (), max(1, total - bound), min(bound, total - 1) + 1)
        return jnp.stack([one, total - one])
    lengths = jnp.asarray(length_profile(count, total, bound, lean), jnp.int32)
    pairs = (count - 1) // 2
    giver, receiver = lengths[1:1 + 2 * pairs:2], lengths[2:2 + 2 * pairs:2]
    margin = jnp.minimum(giver - 1, bound - receiver)
    moved = jax.random.randint(jax.random.fold_in(rng, 1), (pairs,), 0, 1 << 20) % (margin + 1)
    lengths = lengths.at[1:1 + 2 * pairs:2].set(giver - moved).at[2:2 + 2 * pairs:2].set(receiver + moved)
    return lengths[jax.random.permutation(jax.random.fold_in(rng, 2), count)]


def normal_values(stream_key, shape, deviation, limit, shards=(), held_as=jnp.bfloat16):
    values = deviation * jax.random.normal(stream_key, shape, jnp.float32)
    if shards:
        values = values * shard_levels(stream_key, shape, shards, -0.22, 0.18)
    return jnp.clip(values, -limit, limit).astype(held_as)


def setup_inputs(seed: int = 0) -> dict:
    splits = jax.random.split(jax.random.key(seed), 8)
    state = normal_values(splits[0], (LEV, NY, NX), 1.0, 6.0, ((1, 8), (2, 16)), jnp.float32)
    land_mask = place_ends((jax.random.randint(splits[1], (NY, NX), 0, 4) < 3).astype(jnp.int32), jax.random.fold_in(splits[1], 1), 0, 1)
    observations = normal_values(splits[2], (LEV, PROFILES), 1.0, 6.0, ((1, 128),), jnp.float32)
    profile_cells = place_ends(jax.random.randint(splits[3], (PROFILES,), 0, CY * CX), jax.random.fold_in(splits[3], 1), 0, (CY * CX) - 1).astype(jnp.int32)
    profile_counts = jax.vmap(lambda own: uneven(own, DEVICES, PROF_DEV, CAP, 2))(jax.random.split(splits[4], DEVICES)).reshape((DEVICES, DEVICES)).astype(jnp.int32)
    w_in = normal_values(splits[5], (HID, LEV, KS, KS), (LEV * KS * KS) ** -0.5, 0.21875)
    w_out = normal_values(splits[6], (LEV, HID, KS, KS), (HID * KS * KS) ** -0.5, 0.15625)
    return {"state": state, "land_mask": land_mask, "observations": observations, "profile_cells": profile_cells, "profile_counts": profile_counts, "w_in": w_in, "w_out": w_out}


diffusion = 0.2

def round_low(values):
    return lax.optimization_barrier(values.astype(jnp.bfloat16)).astype(jnp.float32)

def pad_grid(values, border):
    padded = jnp.pad(values, ((0, 0), (border, border), (0, 0)))
    return jnp.concatenate([padded[:, :, -border:], padded, padded[:, :, :border]], axis=2)

def laplace(extended, border):
    height = extended.shape[1] - 2 * border
    breadth = extended.shape[2] - 2 * border

    def neighbour(offset_y, offset_x):
        return extended[:, border + offset_y:border + offset_y + height, border + offset_x:border + offset_x + breadth]
    return neighbour(-1, 0) + neighbour(1, 0) + neighbour(0, -1) + neighbour(0, 1) - 4.0 * neighbour(0, 0)

def convolve(padded, kernel):
    return lax.conv_general_dilated(padded[None].astype(jnp.float32), kernel.astype(jnp.float32), (1, 1), 'VALID', dimension_numbers=('NCHW', 'OIHW', 'NCHW'), precision=lax.Precision.HIGHEST)[0]

def flipped(kernel):
    return jnp.transpose(kernel[:, :, ::-1, ::-1], (1, 0, 2, 3))

def kernel_grad(padded, cotangent):
    height, breadth = (cotangent.shape[1], cotangent.shape[2])
    width = padded.shape[2] - breadth + 1
    stripes = []
    for shift_y in range(width):
        pieces = []
        for shift_x in range(width):
            window = padded[:, shift_y:shift_y + height, shift_x:shift_x + breadth]
            pieces.append(jnp.einsum('ohw,chw->oc', cotangent, window, precision=lax.Precision.HIGHEST))
        stripes.append(jnp.stack(pieces, axis=-1))
    return jnp.stack(stripes, axis=-2)

def reference(state, land_mask, observations, profile_cells, profile_counts, w_in, w_out):
    ocean = land_mask.astype(jnp.float32)
    kernel_in = w_in.astype(jnp.float32)
    kernel_out = w_out.astype(jnp.float32)
    current = state
    history = []
    for step_index in range(STEPS):
        coarse = round_low(pad_grid(current, 2))
        activity = jnp.tanh(convolve(coarse, kernel_in))
        hidden = round_low(pad_grid(activity, 2))
        closure = convolve(hidden, kernel_out)
        history.append((coarse, activity, hidden))
        current = current + ocean * (diffusion * laplace(pad_grid(current, 1), 1) + closure)
    finish = jnp.cumsum(profile_counts, axis=1)
    local_rows = jnp.arange(PROF_DEV, dtype=jnp.int32)
    owner_tile = lax.optimization_barrier(jnp.sum((local_rows[None, :, None] >= finish[:, None, :]).astype(jnp.int32), axis=2)).reshape(-1)
    grid_y = owner_tile % N_LAT * CY + profile_cells // CX
    grid_x = owner_tile // N_LAT * CX + profile_cells % CX
    misfits = current[:, grid_y, grid_x] - observations
    misfit = jnp.sum(misfits * misfits) / (2.0 * PROFILES * LEV)
    tangent = jnp.zeros(current.shape, jnp.float32).at[:, grid_y, grid_x].add(misfits / PROF_DEV)
    grad_in = jnp.zeros(w_in.shape, jnp.float32)
    grad_out = jnp.zeros(w_out.shape, jnp.float32)
    for step_index in reversed(range(STEPS)):
        coarse, activity, hidden = history[step_index]
        forcing = ocean * tangent
        forcing_low = round_low(forcing)
        grad_out = grad_out + kernel_grad(hidden, forcing_low)
        spread = convolve(pad_grid(forcing_low, 2), flipped(kernel_out))
        sensitivity = round_low(spread * (1.0 - activity * activity))
        grad_in = grad_in + kernel_grad(coarse, sensitivity)
        tangent = tangent + diffusion * laplace(pad_grid(forcing, 1), 1) + convolve(pad_grid(sensitivity, 2), flipped(kernel_in))
    return (current, misfit, grad_in, grad_out, tangent * PROF_DEV)
```

```python
import jax
import jax.numpy as jnp
from jax import lax
from jax.sharding import PartitionSpec as P

STEPS = 2
CAP = 32


diffusion = 0.2


def extended_2(cells, sides, width):
    for axis, dim in sides:
        count = lax.axis_size(axis)
        head = lax.slice_in_dim(cells, 0, width, axis=dim)
        tail = lax.slice_in_dim(cells, cells.shape[dim] - width, cells.shape[dim], axis=dim)
        cells = jnp.concatenate(
            [
                lax.ppermute(tail, axis, [(i, (i + 1) % count) for i in range(count)]),
                cells,
                lax.ppermute(head, axis, [((i + 1) % count, i) for i in range(count)]),
            ],
            axis=dim,
        )
    return cells


def laplace(extended, border):
    height = extended.shape[1] - 2 * border
    breadth = extended.shape[2] - 2 * border

    def neighbour(offset_y, offset_x):
        return extended[
            :,
            border + offset_y : border + offset_y + height,
            border + offset_x : border + offset_x + breadth,
        ]

    return (
        neighbour(-1, 0)
        + neighbour(1, 0)
        + neighbour(0, -1)
        + neighbour(0, 1)
        - 4.0 * neighbour(0, 0)
    )


def conv_valid(padded, kernel):
    return lax.conv_general_dilated(
        padded[None],
        kernel,
        (1, 1),
        "VALID",
        dimension_numbers=("NCHW", "OIHW", "NCHW"),
        preferred_element_type=jnp.float32,
    )[0]


def flipped(kernel):
    return jnp.transpose(kernel[:, :, ::-1, ::-1], (1, 0, 2, 3))


def kernel_grad(padded, cotangent):
    height, breadth = (cotangent.shape[1], cotangent.shape[2])
    width = padded.shape[2] - breadth + 1
    stripes = []
    for shift_y in range(width):
        pieces = []
        for shift_x in range(width):
            window = padded[:, shift_y : shift_y + height, shift_x : shift_x + breadth]
            pieces.append(
                jnp.einsum("ohw,chw->oc", cotangent, window, preferred_element_type=jnp.float32)
            )
        stripes.append(jnp.stack(pieces, axis=-1))
    return jnp.stack(stripes, axis=-2)


def all_sum(parts, axes):
    count = 1
    for axis in axes:
        count *= lax.axis_size(axis)
    flat = jnp.concatenate([part.reshape(-1) for part in parts])
    size = flat.shape[0]
    chunk = -(-size // count)
    rows = jnp.pad(flat, (0, chunk * count - size)).reshape(count, chunk)
    mine = jnp.sum(lax.all_to_all(rows, axes, 0, 0, tiled=True), axis=0)
    spread = lax.all_to_all(jnp.broadcast_to(mine[None], (count, chunk)), axes, 0, 0, tiled=True)
    flat = spread.reshape(-1)
    sums, offset = [], 0
    for part in parts:
        sums.append(flat[offset : offset + part.size].reshape(part.shape))
        offset += part.size
    return tuple(sums)


def inside_rows(tile_rows, border):
    first_row = lax.axis_index("lat") * tile_rows
    global_rows = first_row + jnp.arange(-border, tile_rows + border, dtype=jnp.int32)
    row_limit = tile_rows * lax.axis_size("lat")
    return ((global_rows >= 0) & (global_rows < row_limit)).astype(jnp.float32)[None, :, None]


def on_device(state, land_mask, observations, profile_cells, profile_counts, w_in, w_out):
    levels, tile_rows, tile_cols = state.shape
    ocean = land_mask.astype(jnp.float32)
    back_in = flipped(w_in)
    back_out = flipped(w_out)
    current = state
    history = []
    for step_index in range(STEPS):
        extended = extended_2(current, (("lon", 2), ("lat", 1)), 4) * inside_rows(tile_rows, 4)
        coarse = extended.astype(jnp.bfloat16)
        activity = jnp.tanh(conv_valid(coarse, w_in))
        hidden = (activity * inside_rows(tile_rows, 2)).astype(jnp.bfloat16)
        closure = conv_valid(hidden, w_out)
        history.append((coarse[:, 2:-2, 2:-2], activity, hidden))
        current = current + ocean * (diffusion * laplace(extended, 4) + closure)
    devices = lax.axis_size("lon") * lax.axis_size("lat")
    profile_dev = observations.shape[1]
    cell_count = tile_rows * tile_cols
    sent_rows = profile_counts[0]
    finish = jnp.cumsum(sent_rows)
    starts = finish - sent_rows
    slot_index = jnp.arange(CAP, dtype=jnp.int32)
    source_row = starts[:, None] + slot_index[None, :]
    filled = (slot_index[None, :] < sent_rows[:, None]).reshape(1, -1)
    picked = jnp.clip(source_row, 0, profile_dev - 1).reshape(-1)
    sent_values = jnp.where(filled, jnp.take(observations, picked, axis=1), 0.0)
    sent_cells = jnp.where(filled, jnp.take(profile_cells, picked)[None, :], cell_count).astype(
        jnp.float32
    )
    payload = jnp.concatenate([sent_values, sent_cells], axis=0)
    arrived = lax.all_to_all(payload, ("lon", "lat"), split_axis=1, concat_axis=1, tiled=True)
    received_values = arrived[:levels]
    received_cells = arrived[levels:].astype(jnp.int32)
    occupied = received_cells < cell_count
    target = jnp.where(occupied, received_cells, 0)[0]
    flat_state = current.reshape(levels, cell_count)
    misfits = jnp.where(occupied, jnp.take(flat_state, target, axis=1) - received_values, 0.0)
    square_sum = jnp.sum(misfits * misfits)
    tangent = (
        jnp.zeros((levels, cell_count), jnp.float32)
        .at[:, target]
        .add(misfits / profile_dev)
        .reshape(levels, tile_rows, tile_cols)
    )
    grad_in = jnp.zeros(w_in.shape, jnp.float32)
    grad_out = jnp.zeros(w_out.shape, jnp.float32)
    for step_index in reversed(range(STEPS)):
        coarse, activity, hidden = history[step_index]
        forcing = ocean * tangent
        forcing_low = forcing.astype(jnp.bfloat16)
        grad_out = grad_out + kernel_grad(hidden, forcing_low)
        derivative = 1.0 - activity * activity
        beside_all = extended_2(forcing, (("lon", 2), ("lat", 1)), 2) * inside_rows(tile_rows, 2)
        spread = conv_valid(beside_all.astype(jnp.bfloat16), back_out)
        sensitivity = (spread * derivative[:, 2:-2, 2:-2]).astype(jnp.bfloat16)
        grad_in = grad_in + kernel_grad(coarse, sensitivity)
        margin = extended_2(sensitivity, (("lon", 2), ("lat", 1)), 2) * inside_rows(
            tile_rows, 2
        ).astype(jnp.bfloat16)
        tangent = tangent + diffusion * laplace(beside_all, 2) + conv_valid(margin, back_in)
    grad_in, grad_out, square_sum = all_sum((grad_in, grad_out, square_sum), ("lon", "lat"))
    misfit = square_sum / (2.0 * profile_dev * devices * levels)
    return (current, misfit, grad_in, grad_out, tangent * profile_dev)


def solution(mesh):
    placed = (
        P(None, "lat", "lon"),
        P("lat", "lon"),
        P(None, ("lon", "lat")),
        P(("lon", "lat")),
        P(("lon", "lat"), None),
        P(),
        P(),
    )
    return jax.shard_map(
        on_device,
        mesh=mesh,
        in_specs=placed,
        out_specs=(P(None, "lat", "lon"), P(), P(), P(), P(None, "lat", "lon")),
        check_vma=False,
    )
```

```python
import jax
import jax.numpy as jnp
from jax import lax
from jax.experimental import pallas as pl
from jax.experimental.pallas import tpu as pltpu
from jax.sharding import PartitionSpec as P

STEPS = 2
CAP = 32


diffusion = 0.2


def extended_2(cells, sides, width):
    for axis, dim in sides:
        count = lax.axis_size(axis)
        head = lax.slice_in_dim(cells, 0, width, axis=dim)
        tail = lax.slice_in_dim(cells, cells.shape[dim] - width, cells.shape[dim], axis=dim)
        cells = jnp.concatenate(
            [
                lax.ppermute(tail, axis, [(i, (i + 1) % count) for i in range(count)]),
                cells,
                lax.ppermute(head, axis, [((i + 1) % count, i) for i in range(count)]),
            ],
            axis=dim,
        )
    return cells


def laplace(extended, border):
    height = extended.shape[1] - 2 * border
    breadth = extended.shape[2] - 2 * border

    def neighbour(offset_y, offset_x):
        return extended[
            :,
            border + offset_y : border + offset_y + height,
            border + offset_x : border + offset_x + breadth,
        ]

    return (
        neighbour(-1, 0)
        + neighbour(1, 0)
        + neighbour(0, -1)
        + neighbour(0, 1)
        - 4.0 * neighbour(0, 0)
    )


def conv_valid(padded, kernel):
    return lax.conv_general_dilated(
        padded[None],
        kernel,
        (1, 1),
        "VALID",
        dimension_numbers=("NCHW", "OIHW", "NCHW"),
        preferred_element_type=jnp.float32,
    )[0]


def flipped(kernel):
    return jnp.transpose(kernel[:, :, ::-1, ::-1], (1, 0, 2, 3))


def kernel_grad(padded, cotangent):
    height, breadth = (cotangent.shape[1], cotangent.shape[2])
    width = padded.shape[2] - breadth + 1
    stripes = []
    for shift_y in range(width):
        pieces = []
        for shift_x in range(width):
            window = padded[:, shift_y : shift_y + height, shift_x : shift_x + breadth]
            pieces.append(
                jnp.einsum("ohw,chw->oc", cotangent, window, preferred_element_type=jnp.float32)
            )
        stripes.append(jnp.stack(pieces, axis=-1))
    return jnp.stack(stripes, axis=-2)


def split3(values):
    high = values.astype(jnp.bfloat16)
    rest = values - high.astype(jnp.float32)
    middle = rest.astype(jnp.bfloat16)
    low = (rest - middle.astype(jnp.float32)).astype(jnp.bfloat16)
    return high, middle, low


def exact_dot(values, onehot):
    high, middle, low = split3(values)
    dims = (((1,), (0,)), ((), ()))
    total = lax.dot_general(high, onehot, dims, preferred_element_type=jnp.float32)
    total = total + lax.dot_general(middle, onehot, dims, preferred_element_type=jnp.float32)
    return total + lax.dot_general(low, onehot, dims, preferred_element_type=jnp.float32)


def pick_columns(values, index, block=512):
    rows, width = values.shape
    count = index.shape[1]

    def body(values_ref, index_ref, out_ref):
        rows_iota = lax.broadcasted_iota(jnp.int32, (width, block), 0)
        onehot = (rows_iota == index_ref[...]).astype(jnp.bfloat16)
        out_ref[...] = exact_dot(values_ref[...], onehot)

    return pl.pallas_call(
        body,
        grid=(count // block,),
        in_specs=[
            pl.BlockSpec((rows, width), lambda i: (0, 0)),
            pl.BlockSpec((1, block), lambda i: (0, i)),
        ],
        out_specs=pl.BlockSpec((rows, block), lambda i: (0, i)),
        out_shape=jax.ShapeDtypeStruct((rows, count), jnp.float32),
        compiler_params=pltpu.CompilerParams(dimension_semantics=("parallel",)),
    )(values, index)


def add_columns(values, index_col, width, block=256):
    rows, count = values.shape

    def body(values_ref, index_ref, out_ref):
        start = pl.program_id(0) * block
        cols_iota = lax.broadcasted_iota(jnp.int32, (count, block), 1) + start
        onehot = (cols_iota == index_ref[...]).astype(jnp.bfloat16)
        out_ref[...] = exact_dot(values_ref[...], onehot)

    return pl.pallas_call(
        body,
        grid=(width // block,),
        in_specs=[
            pl.BlockSpec((rows, count), lambda i: (0, 0)),
            pl.BlockSpec((count, 1), lambda i: (0, 0)),
        ],
        out_specs=pl.BlockSpec((rows, block), lambda i: (0, i)),
        out_shape=jax.ShapeDtypeStruct((rows, width), jnp.float32),
        compiler_params=pltpu.CompilerParams(dimension_semantics=("parallel",)),
    )(values, index_col)


def all_sum(parts, axes):
    count = 1
    for axis in axes:
        count *= lax.axis_size(axis)
    flat = jnp.concatenate([part.reshape(-1) for part in parts])
    size = flat.shape[0]
    chunk = -(-size // count)
    rows = jnp.pad(flat, (0, chunk * count - size)).reshape(count, chunk)
    mine = jnp.sum(lax.all_to_all(rows, axes, 0, 0, tiled=True), axis=0)
    spread = lax.all_to_all(jnp.broadcast_to(mine[None], (count, chunk)), axes, 0, 0, tiled=True)
    flat = spread.reshape(-1)
    sums, offset = [], 0
    for part in parts:
        sums.append(flat[offset : offset + part.size].reshape(part.shape))
        offset += part.size
    return tuple(sums)


def inside_rows(tile_rows, border):
    first_row = lax.axis_index("lat") * tile_rows
    global_rows = first_row + jnp.arange(-border, tile_rows + border, dtype=jnp.int32)
    row_limit = tile_rows * lax.axis_size("lat")
    return ((global_rows >= 0) & (global_rows < row_limit)).astype(jnp.float32)[None, :, None]


def on_device(state, land_mask, observations, profile_cells, profile_counts, w_in, w_out):
    levels, tile_rows, tile_cols = state.shape
    ocean = land_mask.astype(jnp.float32)
    back_in = flipped(w_in)
    back_out = flipped(w_out)
    current = state
    history = []
    for step_index in range(STEPS):
        extended = extended_2(current, (("lon", 2), ("lat", 1)), 4) * inside_rows(tile_rows, 4)
        coarse = extended.astype(jnp.bfloat16)
        activity = jnp.tanh(conv_valid(coarse, w_in))
        hidden = (activity * inside_rows(tile_rows, 2)).astype(jnp.bfloat16)
        closure = conv_valid(hidden, w_out)
        history.append((coarse[:, 2:-2, 2:-2], activity, hidden))
        current = current + ocean * (diffusion * laplace(extended, 4) + closure)
    devices = lax.axis_size("lon") * lax.axis_size("lat")
    profile_dev = observations.shape[1]
    cell_count = tile_rows * tile_cols
    sent_rows = profile_counts[0]
    finish = jnp.cumsum(sent_rows)
    starts = finish - sent_rows
    slot_index = jnp.arange(CAP, dtype=jnp.int32)
    source_row = starts[:, None] + slot_index[None, :]
    filled = (slot_index[None, :] < sent_rows[:, None]).reshape(1, -1)
    picked = jnp.where(filled, source_row.reshape(1, -1), profile_dev)
    source = jnp.concatenate(
        [observations, profile_cells[None, :].astype(jnp.float32)], axis=0
    )
    gathered = pick_columns(source, picked)
    sent_values = gathered[:levels]
    sent_cells = jnp.where(filled, gathered[levels:], float(cell_count))
    payload = jnp.concatenate([sent_values, sent_cells], axis=0)
    arrived = lax.all_to_all(payload, ("lon", "lat"), split_axis=1, concat_axis=1, tiled=True)
    received_values = arrived[:levels]
    received_cells = arrived[levels:].astype(jnp.int32)
    occupied = received_cells < cell_count
    target = jnp.where(occupied, received_cells, cell_count)
    flat_state = current.reshape(levels, cell_count)
    misfits = jnp.where(occupied, pick_columns(flat_state, target) - received_values, 0.0)
    square_sum = jnp.sum(misfits * misfits)
    tangent = add_columns(misfits / profile_dev, target.reshape(-1, 1), cell_count).reshape(
        levels, tile_rows, tile_cols
    )
    grad_in = jnp.zeros(w_in.shape, jnp.float32)
    grad_out = jnp.zeros(w_out.shape, jnp.float32)
    for step_index in reversed(range(STEPS)):
        coarse, activity, hidden = history[step_index]
        forcing = ocean * tangent
        forcing_low = forcing.astype(jnp.bfloat16)
        grad_out = grad_out + kernel_grad(hidden, forcing_low)
        derivative = 1.0 - activity * activity
        beside_all = extended_2(forcing, (("lon", 2), ("lat", 1)), 2) * inside_rows(tile_rows, 2)
        spread = conv_valid(beside_all.astype(jnp.bfloat16), back_out)
        sensitivity = (spread * derivative[:, 2:-2, 2:-2]).astype(jnp.bfloat16)
        grad_in = grad_in + kernel_grad(coarse, sensitivity)
        margin = extended_2(sensitivity, (("lon", 2), ("lat", 1)), 2) * inside_rows(
            tile_rows, 2
        ).astype(jnp.bfloat16)
        tangent = tangent + diffusion * laplace(beside_all, 2) + conv_valid(margin, back_in)
    grad_in, grad_out, square_sum = all_sum((grad_in, grad_out, square_sum), ("lon", "lat"))
    misfit = square_sum / (2.0 * profile_dev * devices * levels)
    return (current, misfit, grad_in, grad_out, tangent * profile_dev)


def solution(mesh):
    placed = (
        P(None, "lat", "lon"),
        P("lat", "lon"),
        P(None, ("lon", "lat")),
        P(("lon", "lat")),
        P(("lon", "lat"), None),
        P(),
        P(),
    )
    return jax.shard_map(
        on_device,
        mesh=mesh,
        in_specs=placed,
        out_specs=(P(None, "lat", "lon"), P(), P(), P(), P(None, "lat", "lon")),
        check_vma=False,
    )
```

```python
import jax
import jax.numpy as jnp
from jax import lax
from jax.experimental import pallas as pl
from jax.experimental.pallas import tpu as pltpu
from jax.sharding import PartitionSpec as P

STEPS = 2
CAP = 32


diffusion = 0.2


def extended_2(cells, sides, width):
    for axis, dim in sides:
        count = lax.axis_size(axis)
        head = lax.slice_in_dim(cells, 0, width, axis=dim)
        tail = lax.slice_in_dim(cells, cells.shape[dim] - width, cells.shape[dim], axis=dim)
        cells = jnp.concatenate(
            [
                lax.ppermute(tail, axis, [(i, (i + 1) % count) for i in range(count)]),
                cells,
                lax.ppermute(head, axis, [((i + 1) % count, i) for i in range(count)]),
            ],
            axis=dim,
        )
    return cells


def laplace(extended, border):
    height = extended.shape[1] - 2 * border
    breadth = extended.shape[2] - 2 * border

    def neighbour(offset_y, offset_x):
        return extended[
            :,
            border + offset_y : border + offset_y + height,
            border + offset_x : border + offset_x + breadth,
        ]

    return (
        neighbour(-1, 0)
        + neighbour(1, 0)
        + neighbour(0, -1)
        + neighbour(0, 1)
        - 4.0 * neighbour(0, 0)
    )


def conv_valid(padded, kernel):
    return lax.conv_general_dilated(
        padded[None],
        kernel,
        (1, 1),
        "VALID",
        dimension_numbers=("NCHW", "OIHW", "NCHW"),
        preferred_element_type=jnp.float32,
    )[0]


def flipped(kernel):
    return jnp.transpose(kernel[:, :, ::-1, ::-1], (1, 0, 2, 3))


def kernel_grad(padded, cotangent):
    height, breadth = (cotangent.shape[1], cotangent.shape[2])
    width = padded.shape[2] - breadth + 1
    stripes = []
    for shift_y in range(width):
        pieces = []
        for shift_x in range(width):
            window = padded[:, shift_y : shift_y + height, shift_x : shift_x + breadth]
            pieces.append(
                jnp.einsum("ohw,chw->oc", cotangent, window, preferred_element_type=jnp.float32)
            )
        stripes.append(jnp.stack(pieces, axis=-1))
    return jnp.stack(stripes, axis=-2)


def split3(values):
    high = values.astype(jnp.bfloat16)
    rest = values - high.astype(jnp.float32)
    middle = rest.astype(jnp.bfloat16)
    low = (rest - middle.astype(jnp.float32)).astype(jnp.bfloat16)
    return high, middle, low


def exact_dot(values, onehot):
    high, middle, low = split3(values)
    dims = (((1,), (0,)), ((), ()))
    total = lax.dot_general(high, onehot, dims, preferred_element_type=jnp.float32)
    total = total + lax.dot_general(middle, onehot, dims, preferred_element_type=jnp.float32)
    return total + lax.dot_general(low, onehot, dims, preferred_element_type=jnp.float32)


def pick_columns(values, index, block=512):
    rows, width = values.shape
    count = index.shape[1]

    def body(values_ref, index_ref, out_ref):
        rows_iota = lax.broadcasted_iota(jnp.int32, (width, block), 0)
        onehot = (rows_iota == index_ref[...]).astype(jnp.bfloat16)
        out_ref[...] = exact_dot(values_ref[...], onehot)

    return pl.pallas_call(
        body,
        grid=(count // block,),
        in_specs=[
            pl.BlockSpec((rows, width), lambda i: (0, 0)),
            pl.BlockSpec((1, block), lambda i: (0, i)),
        ],
        out_specs=pl.BlockSpec((rows, block), lambda i: (0, i)),
        out_shape=jax.ShapeDtypeStruct((rows, count), jnp.float32),
        compiler_params=pltpu.CompilerParams(dimension_semantics=("parallel",)),
    )(values, index)


def pick_cells(values, where_to, block=512):
    levels, rows, cols = values.shape
    count = where_to.shape[1]

    def body(values_ref, where_ref, out_ref):
        row_of = where_ref[0:1, :]
        col_of = where_ref[1:2, :]
        cols_iota = lax.broadcasted_iota(jnp.int32, (cols, block), 0)
        onehot = (cols_iota == col_of).astype(jnp.bfloat16)
        total = jnp.zeros((levels, block), jnp.float32)
        for row in range(rows):
            picked = exact_dot(values_ref[:, row, :], onehot)
            total = total + jnp.where(row_of == row, picked, 0.0)
        out_ref[...] = total

    return pl.pallas_call(
        body,
        grid=(count // block,),
        in_specs=[
            pl.BlockSpec((levels, rows, cols), lambda i: (0, 0, 0)),
            pl.BlockSpec((2, block), lambda i: (0, i)),
        ],
        out_specs=pl.BlockSpec((levels, block), lambda i: (0, i)),
        out_shape=jax.ShapeDtypeStruct((levels, count), jnp.float32),
        compiler_params=pltpu.CompilerParams(dimension_semantics=("parallel",)),
    )(values, where_to)


def add_columns(values, index_col, width, block=256):
    rows, count = values.shape

    def body(values_ref, index_ref, out_ref):
        start = pl.program_id(0) * block
        cols_iota = lax.broadcasted_iota(jnp.int32, (count, block), 1) + start
        onehot = (cols_iota == index_ref[...]).astype(jnp.bfloat16)
        out_ref[...] = exact_dot(values_ref[...], onehot)

    return pl.pallas_call(
        body,
        grid=(width // block,),
        in_specs=[
            pl.BlockSpec((rows, count), lambda i: (0, 0)),
            pl.BlockSpec((count, 1), lambda i: (0, 0)),
        ],
        out_specs=pl.BlockSpec((rows, block), lambda i: (0, i)),
        out_shape=jax.ShapeDtypeStruct((rows, width), jnp.float32),
        compiler_params=pltpu.CompilerParams(dimension_semantics=("parallel",)),
    )(values, index_col)


def all_sum(parts, axes):
    count = 1
    for axis in axes:
        count *= lax.axis_size(axis)
    flat = jnp.concatenate([part.reshape(-1) for part in parts])
    size = flat.shape[0]
    chunk = -(-size // count)
    rows = jnp.pad(flat, (0, chunk * count - size)).reshape(count, chunk)
    mine = jnp.sum(lax.all_to_all(rows, axes, 0, 0, tiled=True), axis=0)
    spread = lax.all_to_all(jnp.broadcast_to(mine[None], (count, chunk)), axes, 0, 0, tiled=True)
    flat = spread.reshape(-1)
    sums, offset = [], 0
    for part in parts:
        sums.append(flat[offset : offset + part.size].reshape(part.shape))
        offset += part.size
    return tuple(sums)


def inside_rows(tile_rows, border):
    first_row = lax.axis_index("lat") * tile_rows
    global_rows = first_row + jnp.arange(-border, tile_rows + border, dtype=jnp.int32)
    row_limit = tile_rows * lax.axis_size("lat")
    return ((global_rows >= 0) & (global_rows < row_limit)).astype(jnp.float32)[None, :, None]


def on_device(state, land_mask, observations, profile_cells, profile_counts, w_in, w_out):
    levels, tile_rows, tile_cols = state.shape
    ocean = land_mask.astype(jnp.float32)
    back_in = flipped(w_in)
    back_out = flipped(w_out)
    current = state
    history = []
    for step_index in range(STEPS):
        extended = extended_2(current, (("lon", 2), ("lat", 1)), 4) * inside_rows(tile_rows, 4)
        coarse = extended.astype(jnp.bfloat16)
        activity = jnp.tanh(conv_valid(coarse, w_in))
        hidden = (activity * inside_rows(tile_rows, 2)).astype(jnp.bfloat16)
        closure = conv_valid(hidden, w_out)
        history.append((coarse[:, 2:-2, 2:-2], activity, hidden))
        current = current + ocean * (diffusion * laplace(extended, 4) + closure)
    devices = lax.axis_size("lon") * lax.axis_size("lat")
    profile_dev = observations.shape[1]
    cell_count = tile_rows * tile_cols
    sent_rows = profile_counts[0]
    finish = jnp.cumsum(sent_rows)
    starts = finish - sent_rows
    slot_index = jnp.arange(CAP, dtype=jnp.int32)
    source_row = starts[:, None] + slot_index[None, :]
    filled = (slot_index[None, :] < sent_rows[:, None]).reshape(1, -1)
    picked = jnp.where(filled, source_row.reshape(1, -1), profile_dev)
    source = jnp.concatenate(
        [observations, profile_cells[None, :].astype(jnp.float32)], axis=0
    )
    gathered = pick_columns(source, picked)
    sent_values = gathered[:levels]
    sent_cells = jnp.where(filled, gathered[levels:], float(cell_count))
    payload = jnp.concatenate([sent_values, sent_cells], axis=0)
    arrived = lax.all_to_all(payload, ("lon", "lat"), split_axis=1, concat_axis=1, tiled=True)
    received_values = arrived[:levels]
    received_cells = arrived[levels:].astype(jnp.int32)
    occupied = received_cells < cell_count
    target = jnp.where(occupied, received_cells, cell_count)
    flat_state = current.reshape(levels, cell_count)
    misfits = jnp.where(occupied, jnp.take(flat_state, target[0], axis=1, mode="clip") - received_values, 0.0)
    square_sum = jnp.sum(misfits * misfits)
    tangent = jnp.zeros((levels, cell_count), jnp.float32).at[:, jnp.where(occupied, target, 0)[0]].add(misfits / profile_dev).reshape(
        levels, tile_rows, tile_cols
    )
    grad_in = jnp.zeros(w_in.shape, jnp.float32)
    grad_out = jnp.zeros(w_out.shape, jnp.float32)
    for step_index in reversed(range(STEPS)):
        coarse, activity, hidden = history[step_index]
        forcing = ocean * tangent
        forcing_low = forcing.astype(jnp.bfloat16)
        grad_out = grad_out + kernel_grad(hidden, forcing_low)
        derivative = 1.0 - activity * activity
        beside_all = extended_2(forcing, (("lon", 2), ("lat", 1)), 2) * inside_rows(tile_rows, 2)
        spread = conv_valid(beside_all.astype(jnp.bfloat16), back_out)
        sensitivity = (spread * derivative[:, 2:-2, 2:-2]).astype(jnp.bfloat16)
        grad_in = grad_in + kernel_grad(coarse, sensitivity)
        margin = extended_2(sensitivity, (("lon", 2), ("lat", 1)), 2) * inside_rows(
            tile_rows, 2
        ).astype(jnp.bfloat16)
        tangent = tangent + diffusion * laplace(beside_all, 2) + conv_valid(margin, back_in)
    grad_in, grad_out, square_sum = all_sum((grad_in, grad_out, square_sum), ("lon", "lat"))
    misfit = square_sum / (2.0 * profile_dev * devices * levels)
    return (current, misfit, grad_in, grad_out, tangent * profile_dev)


def solution(mesh):
    placed = (
        P(None, "lat", "lon"),
        P("lat", "lon"),
        P(None, ("lon", "lat")),
        P(("lon", "lat")),
        P(("lon", "lat"), None),
        P(),
        P(),
    )
    return jax.shard_map(
        on_device,
        mesh=mesh,
        in_specs=placed,
        out_specs=(P(None, "lat", "lon"), P(), P(), P(), P(None, "lat", "lon")),
        check_vma=False,
    )
```

```python
import jax
import jax.numpy as jnp
from jax import lax
from jax.experimental import pallas as pl
from jax.experimental.pallas import tpu as pltpu
from jax.sharding import PartitionSpec as P

STEPS = 2
CAP = 32


diffusion = 0.2


def extended_2(cells, width):
    n_lon = lax.axis_size("lon")
    n_lat = lax.axis_size("lat")

    def shift(block, d_lon, d_lat):
        pairs = []
        for i in range(n_lon):
            for j in range(n_lat):
                if 0 <= j + d_lat < n_lat:
                    pairs.append((i * n_lat + j, ((i + d_lon) % n_lon) * n_lat + j + d_lat))
        return lax.ppermute(block, ("lon", "lat"), pairs)

    rows, cols = cells.shape[1], cells.shape[2]
    low_rows, high_rows = cells[:, rows - width :], cells[:, :width]
    top = jnp.concatenate(
        [
            shift(low_rows[:, :, cols - width :], 1, 1),
            shift(low_rows, 0, 1),
            shift(low_rows[:, :, :width], -1, 1),
        ],
        axis=2,
    )
    middle = jnp.concatenate(
        [shift(cells[:, :, cols - width :], 1, 0), cells, shift(cells[:, :, :width], -1, 0)],
        axis=2,
    )
    bottom = jnp.concatenate(
        [
            shift(high_rows[:, :, cols - width :], 1, -1),
            shift(high_rows, 0, -1),
            shift(high_rows[:, :, :width], -1, -1),
        ],
        axis=2,
    )
    return jnp.concatenate([top, middle, bottom], axis=1)


def laplace(extended, border):
    height = extended.shape[1] - 2 * border
    breadth = extended.shape[2] - 2 * border

    def neighbour(offset_y, offset_x):
        return extended[
            :,
            border + offset_y : border + offset_y + height,
            border + offset_x : border + offset_x + breadth,
        ]

    return (
        neighbour(-1, 0)
        + neighbour(1, 0)
        + neighbour(0, -1)
        + neighbour(0, 1)
        - 4.0 * neighbour(0, 0)
    )


def conv_valid(padded, kernel):
    return lax.conv_general_dilated(
        padded[None],
        kernel,
        (1, 1),
        "VALID",
        dimension_numbers=("NCHW", "OIHW", "NCHW"),
        preferred_element_type=jnp.float32,
    )[0]


def flipped(kernel):
    return jnp.transpose(kernel[:, :, ::-1, ::-1], (1, 0, 2, 3))


def kernel_grad(padded, cotangent):
    height, breadth = (cotangent.shape[1], cotangent.shape[2])
    width = padded.shape[2] - breadth + 1
    stripes = []
    for shift_y in range(width):
        pieces = []
        for shift_x in range(width):
            window = padded[:, shift_y : shift_y + height, shift_x : shift_x + breadth]
            pieces.append(
                jnp.einsum("ohw,chw->oc", cotangent, window, preferred_element_type=jnp.float32)
            )
        stripes.append(jnp.stack(pieces, axis=-1))
    return jnp.stack(stripes, axis=-2)


def split3(values):
    high = values.astype(jnp.bfloat16)
    rest = values - high.astype(jnp.float32)
    middle = rest.astype(jnp.bfloat16)
    low = (rest - middle.astype(jnp.float32)).astype(jnp.bfloat16)
    return high, middle, low


def exact_dot(values, onehot):
    high, middle, low = split3(values)
    dims = (((1,), (0,)), ((), ()))
    total = lax.dot_general(high, onehot, dims, preferred_element_type=jnp.float32)
    total = total + lax.dot_general(middle, onehot, dims, preferred_element_type=jnp.float32)
    return total + lax.dot_general(low, onehot, dims, preferred_element_type=jnp.float32)


def pick_columns(values, index, block=512):
    rows, width = values.shape
    count = index.shape[1]

    def body(values_ref, index_ref, out_ref):
        rows_iota = lax.broadcasted_iota(jnp.int32, (width, block), 0)
        onehot = (rows_iota == index_ref[...]).astype(jnp.bfloat16)
        out_ref[...] = exact_dot(values_ref[...], onehot)

    return pl.pallas_call(
        body,
        grid=(count // block,),
        in_specs=[
            pl.BlockSpec((rows, width), lambda i: (0, 0)),
            pl.BlockSpec((1, block), lambda i: (0, i)),
        ],
        out_specs=pl.BlockSpec((rows, block), lambda i: (0, i)),
        out_shape=jax.ShapeDtypeStruct((rows, count), jnp.float32),
        compiler_params=pltpu.CompilerParams(dimension_semantics=("parallel",)),
    )(values, index)


def pick_cells(values, where_to, block=512):
    levels, rows, cols = values.shape
    count = where_to.shape[1]

    def body(values_ref, where_ref, out_ref):
        row_of = where_ref[0:1, :]
        col_of = where_ref[1:2, :]
        cols_iota = lax.broadcasted_iota(jnp.int32, (cols, block), 0)
        onehot = (cols_iota == col_of).astype(jnp.bfloat16)
        total = jnp.zeros((levels, block), jnp.float32)
        for row in range(rows):
            picked = exact_dot(values_ref[:, row, :], onehot)
            total = total + jnp.where(row_of == row, picked, 0.0)
        out_ref[...] = total

    return pl.pallas_call(
        body,
        grid=(count // block,),
        in_specs=[
            pl.BlockSpec((levels, rows, cols), lambda i: (0, 0, 0)),
            pl.BlockSpec((2, block), lambda i: (0, i)),
        ],
        out_specs=pl.BlockSpec((levels, block), lambda i: (0, i)),
        out_shape=jax.ShapeDtypeStruct((levels, count), jnp.float32),
        compiler_params=pltpu.CompilerParams(dimension_semantics=("parallel",)),
    )(values, where_to)


def add_columns(values, index_col, width, block=256):
    rows, count = values.shape

    def body(values_ref, index_ref, out_ref):
        start = pl.program_id(0) * block
        cols_iota = lax.broadcasted_iota(jnp.int32, (count, block), 1) + start
        onehot = (cols_iota == index_ref[...]).astype(jnp.bfloat16)
        out_ref[...] = exact_dot(values_ref[...], onehot)

    return pl.pallas_call(
        body,
        grid=(width // block,),
        in_specs=[
            pl.BlockSpec((rows, count), lambda i: (0, 0)),
            pl.BlockSpec((count, 1), lambda i: (0, 0)),
        ],
        out_specs=pl.BlockSpec((rows, block), lambda i: (0, i)),
        out_shape=jax.ShapeDtypeStruct((rows, width), jnp.float32),
        compiler_params=pltpu.CompilerParams(dimension_semantics=("parallel",)),
    )(values, index_col)


def all_sum(parts, axes):
    count = 1
    for axis in axes:
        count *= lax.axis_size(axis)
    flat = jnp.concatenate([part.reshape(-1) for part in parts])
    size = flat.shape[0]
    chunk = -(-size // count)
    rows = jnp.pad(flat, (0, chunk * count - size)).reshape(count, chunk)
    mine = jnp.sum(lax.all_to_all(rows, axes, 0, 0, tiled=True), axis=0)
    spread = lax.all_to_all(jnp.broadcast_to(mine[None], (count, chunk)), axes, 0, 0, tiled=True)
    flat = spread.reshape(-1)
    sums, offset = [], 0
    for part in parts:
        sums.append(flat[offset : offset + part.size].reshape(part.shape))
        offset += part.size
    return tuple(sums)


def inside_rows(tile_rows, border):
    first_row = lax.axis_index("lat") * tile_rows
    global_rows = first_row + jnp.arange(-border, tile_rows + border, dtype=jnp.int32)
    row_limit = tile_rows * lax.axis_size("lat")
    return ((global_rows >= 0) & (global_rows < row_limit)).astype(jnp.float32)[None, :, None]


def on_device(state, land_mask, observations, profile_cells, profile_counts, w_in, w_out):
    levels, tile_rows, tile_cols = state.shape
    ocean = land_mask.astype(jnp.float32)
    back_in = flipped(w_in)
    back_out = flipped(w_out)
    current = state
    history = []
    for step_index in range(STEPS):
        extended = extended_2(current, 4)
        coarse = extended.astype(jnp.bfloat16)
        activity = jnp.tanh(conv_valid(coarse, w_in))
        hidden = (activity * inside_rows(tile_rows, 2)).astype(jnp.bfloat16)
        closure = conv_valid(hidden, w_out)
        history.append((coarse[:, 2:-2, 2:-2], activity, hidden))
        current = current + ocean * (diffusion * laplace(extended, 4) + closure)
    devices = lax.axis_size("lon") * lax.axis_size("lat")
    profile_dev = observations.shape[1]
    cell_count = tile_rows * tile_cols
    sent_rows = profile_counts[0]
    finish = jnp.cumsum(sent_rows)
    starts = finish - sent_rows
    slot_index = jnp.arange(CAP, dtype=jnp.int32)
    source_row = starts[:, None] + slot_index[None, :]
    filled = (slot_index[None, :] < sent_rows[:, None]).reshape(1, -1)
    picked = jnp.where(filled, source_row.reshape(1, -1), profile_dev)
    source = jnp.concatenate(
        [observations, profile_cells[None, :].astype(jnp.float32)], axis=0
    )
    gathered = pick_columns(source, picked)
    sent_values = gathered[:levels]
    sent_cells = jnp.where(filled, gathered[levels:], float(cell_count))
    payload = jnp.concatenate([sent_values, sent_cells], axis=0)
    arrived = lax.all_to_all(payload, ("lon", "lat"), split_axis=1, concat_axis=1, tiled=True)
    received_values = arrived[:levels]
    received_cells = arrived[levels:].astype(jnp.int32)
    occupied = received_cells < cell_count
    target = jnp.where(occupied, received_cells, cell_count)
    flat_state = current.reshape(levels, cell_count)
    misfits = jnp.where(occupied, jnp.take(flat_state, target[0], axis=1, mode="clip") - received_values, 0.0)
    square_sum = jnp.sum(misfits * misfits)
    tangent = jnp.zeros((levels, cell_count), jnp.float32).at[:, jnp.where(occupied, target, 0)[0]].add(misfits / profile_dev).reshape(
        levels, tile_rows, tile_cols
    )
    grad_in = jnp.zeros(w_in.shape, jnp.float32)
    grad_out = jnp.zeros(w_out.shape, jnp.float32)
    for step_index in reversed(range(STEPS)):
        coarse, activity, hidden = history[step_index]
        forcing = ocean * tangent
        forcing_low = forcing.astype(jnp.bfloat16)
        grad_out = grad_out + kernel_grad(hidden, forcing_low)
        derivative = 1.0 - activity * activity
        beside_all = extended_2(forcing, 2)
        spread = conv_valid(beside_all.astype(jnp.bfloat16), back_out)
        sensitivity = (spread * derivative[:, 2:-2, 2:-2]).astype(jnp.bfloat16)
        grad_in = grad_in + kernel_grad(coarse, sensitivity)
        margin = extended_2(sensitivity, 2)
        tangent = tangent + diffusion * laplace(beside_all, 2) + conv_valid(margin, back_in)
    grad_in, grad_out, square_sum = all_sum((grad_in, grad_out, square_sum), ("lon", "lat"))
    misfit = square_sum / (2.0 * profile_dev * devices * levels)
    return (current, misfit, grad_in, grad_out, tangent * profile_dev)


def solution(mesh):
    placed = (
        P(None, "lat", "lon"),
        P("lat", "lon"),
        P(None, ("lon", "lat")),
        P(("lon", "lat")),
        P(("lon", "lat"), None),
        P(),
        P(),
    )
    return jax.shard_map(
        on_device,
        mesh=mesh,
        in_specs=placed,
        out_specs=(P(None, "lat", "lon"), P(), P(), P(), P(None, "lat", "lon")),
        check_vma=False,
    )
```

```python
import jax
import jax.numpy as jnp
from jax import lax
from jax.experimental import pallas as pl
from jax.experimental.pallas import tpu as pltpu
from jax.sharding import PartitionSpec as P

STEPS = 2
CAP = 32


diffusion = 0.2


def extended_2(cells, sides, width):
    for axis, dim in sides:
        count = lax.axis_size(axis)
        head = lax.slice_in_dim(cells, 0, width, axis=dim)
        tail = lax.slice_in_dim(cells, cells.shape[dim] - width, cells.shape[dim], axis=dim)
        cells = jnp.concatenate(
            [
                lax.ppermute(tail, axis, [(i, (i + 1) % count) for i in range(count)]),
                cells,
                lax.ppermute(head, axis, [((i + 1) % count, i) for i in range(count)]),
            ],
            axis=dim,
        )
    return cells


def laplace(extended, border):
    height = extended.shape[1] - 2 * border
    breadth = extended.shape[2] - 2 * border

    def neighbour(offset_y, offset_x):
        return extended[
            :,
            border + offset_y : border + offset_y + height,
            border + offset_x : border + offset_x + breadth,
        ]

    return (
        neighbour(-1, 0)
        + neighbour(1, 0)
        + neighbour(0, -1)
        + neighbour(0, 1)
        - 4.0 * neighbour(0, 0)
    )


def conv_valid(padded, kernel):
    return lax.conv_general_dilated(
        padded[None],
        kernel,
        (1, 1),
        "VALID",
        dimension_numbers=("NCHW", "OIHW", "NCHW"),
        preferred_element_type=jnp.float32,
    )[0]


def flipped(kernel):
    return jnp.transpose(kernel[:, :, ::-1, ::-1], (1, 0, 2, 3))


def kernel_grad(padded, cotangent):
    height, breadth = (cotangent.shape[1], cotangent.shape[2])
    width = padded.shape[2] - breadth + 1
    stripes = []
    for shift_y in range(width):
        pieces = []
        for shift_x in range(width):
            window = padded[:, shift_y : shift_y + height, shift_x : shift_x + breadth]
            pieces.append(
                jnp.einsum("ohw,chw->oc", cotangent, window, preferred_element_type=jnp.float32)
            )
        stripes.append(jnp.stack(pieces, axis=-1))
    return jnp.stack(stripes, axis=-2)


def split3(values):
    high = values.astype(jnp.bfloat16)
    rest = values - high.astype(jnp.float32)
    middle = rest.astype(jnp.bfloat16)
    low = (rest - middle.astype(jnp.float32)).astype(jnp.bfloat16)
    return high, middle, low


def exact_dot(values, onehot):
    high, middle, low = split3(values)
    dims = (((1,), (0,)), ((), ()))
    total = lax.dot_general(high, onehot, dims, preferred_element_type=jnp.float32)
    total = total + lax.dot_general(middle, onehot, dims, preferred_element_type=jnp.float32)
    return total + lax.dot_general(low, onehot, dims, preferred_element_type=jnp.float32)


def pick_columns(values, index, block=512):
    rows, width = values.shape
    count = index.shape[1]

    def body(values_ref, index_ref, out_ref):
        rows_iota = lax.broadcasted_iota(jnp.int32, (width, block), 0)
        onehot = (rows_iota == index_ref[...]).astype(jnp.bfloat16)
        out_ref[...] = exact_dot(values_ref[...], onehot)

    return pl.pallas_call(
        body,
        grid=(count // block,),
        in_specs=[
            pl.BlockSpec((rows, width), lambda i: (0, 0)),
            pl.BlockSpec((1, block), lambda i: (0, i)),
        ],
        out_specs=pl.BlockSpec((rows, block), lambda i: (0, i)),
        out_shape=jax.ShapeDtypeStruct((rows, count), jnp.float32),
        compiler_params=pltpu.CompilerParams(dimension_semantics=("parallel",)),
    )(values, index)


def pick_cells(values, where_to, block=512):
    levels, rows, cols = values.shape
    count = where_to.shape[1]

    def body(values_ref, where_ref, out_ref):
        row_of = where_ref[0:1, :]
        col_of = where_ref[1:2, :]
        cols_iota = lax.broadcasted_iota(jnp.int32, (cols, block), 0)
        onehot = (cols_iota == col_of).astype(jnp.bfloat16)
        total = jnp.zeros((levels, block), jnp.float32)
        for row in range(rows):
            picked = exact_dot(values_ref[:, row, :], onehot)
            total = total + jnp.where(row_of == row, picked, 0.0)
        out_ref[...] = total

    return pl.pallas_call(
        body,
        grid=(count // block,),
        in_specs=[
            pl.BlockSpec((levels, rows, cols), lambda i: (0, 0, 0)),
            pl.BlockSpec((2, block), lambda i: (0, i)),
        ],
        out_specs=pl.BlockSpec((levels, block), lambda i: (0, i)),
        out_shape=jax.ShapeDtypeStruct((levels, count), jnp.float32),
        compiler_params=pltpu.CompilerParams(dimension_semantics=("parallel",)),
    )(values, where_to)


def add_columns(values, index_col, width, block=256):
    rows, count = values.shape

    def body(values_ref, index_ref, out_ref):
        start = pl.program_id(0) * block
        cols_iota = lax.broadcasted_iota(jnp.int32, (count, block), 1) + start
        onehot = (cols_iota == index_ref[...]).astype(jnp.bfloat16)
        out_ref[...] = exact_dot(values_ref[...], onehot)

    return pl.pallas_call(
        body,
        grid=(width // block,),
        in_specs=[
            pl.BlockSpec((rows, count), lambda i: (0, 0)),
            pl.BlockSpec((count, 1), lambda i: (0, 0)),
        ],
        out_specs=pl.BlockSpec((rows, block), lambda i: (0, i)),
        out_shape=jax.ShapeDtypeStruct((rows, width), jnp.float32),
        compiler_params=pltpu.CompilerParams(dimension_semantics=("parallel",)),
    )(values, index_col)


def all_sum(parts, axes):
    count = 1
    for axis in axes:
        count *= lax.axis_size(axis)
    flat = jnp.concatenate([part.reshape(-1) for part in parts])
    size = flat.shape[0]
    chunk = -(-size // count)
    rows = jnp.pad(flat, (0, chunk * count - size)).reshape(count, chunk)
    mine = jnp.sum(lax.all_to_all(rows, axes, 0, 0, tiled=True), axis=0)
    spread = lax.all_to_all(jnp.broadcast_to(mine[None], (count, chunk)), axes, 0, 0, tiled=True)
    flat = spread.reshape(-1)
    sums, offset = [], 0
    for part in parts:
        sums.append(flat[offset : offset + part.size].reshape(part.shape))
        offset += part.size
    return tuple(sums)


def inside_rows(tile_rows, border):
    first_row = lax.axis_index("lat") * tile_rows
    global_rows = first_row + jnp.arange(-border, tile_rows + border, dtype=jnp.int32)
    row_limit = tile_rows * lax.axis_size("lat")
    return ((global_rows >= 0) & (global_rows < row_limit)).astype(jnp.float32)[None, :, None]


def on_device(state, land_mask, observations, profile_cells, profile_counts, w_in, w_out):
    levels, tile_rows, tile_cols = state.shape
    ocean = land_mask.astype(jnp.float32)
    back_in = flipped(w_in)
    back_out = flipped(w_out)
    current = state
    history = []
    for step_index in range(STEPS):
        extended = extended_2(current, (("lon", 2), ("lat", 1)), 4) * inside_rows(tile_rows, 4)
        coarse = extended.astype(jnp.bfloat16)
        activity = jnp.tanh(conv_valid(coarse, w_in))
        hidden = (activity * inside_rows(tile_rows, 2)).astype(jnp.bfloat16)
        closure = conv_valid(hidden, w_out)
        history.append((coarse[:, 2:-2, 2:-2], activity, hidden))
        current = current + ocean * (diffusion * laplace(extended, 4) + closure)
    devices = lax.axis_size("lon") * lax.axis_size("lat")
    profile_dev = observations.shape[1]
    cell_count = tile_rows * tile_cols
    sent_rows = profile_counts[0]
    finish = jnp.cumsum(sent_rows)
    starts = finish - sent_rows
    slot_index = jnp.arange(CAP, dtype=jnp.int32)
    source_row = starts[:, None] + slot_index[None, :]
    filled = (slot_index[None, :] < sent_rows[:, None]).reshape(1, -1)
    picked = jnp.where(filled, source_row.reshape(1, -1), profile_dev)
    source = jnp.concatenate(
        [observations, profile_cells[None, :].astype(jnp.float32)], axis=0
    )
    gathered = pick_columns(source, picked)
    sent_values = gathered[:levels]
    sent_cells = jnp.where(filled, gathered[levels:], float(cell_count))
    payload = jnp.concatenate([sent_values, sent_cells], axis=0)
    arrived = lax.all_to_all(payload, ("lon", "lat"), split_axis=1, concat_axis=1, tiled=True)
    received_values = arrived[:levels]
    received_cells = arrived[levels:].astype(jnp.int32)
    occupied = received_cells < cell_count
    target = jnp.where(occupied, received_cells, cell_count)
    flat_state = current.reshape(levels, cell_count)
    misfits = jnp.where(occupied, jnp.take(flat_state, target[0], axis=1, mode="clip") - received_values, 0.0)
    square_sum = jnp.sum(misfits * misfits)
    tangent = jnp.zeros((levels, cell_count), jnp.float32).at[:, jnp.where(occupied, target, 0)[0]].add(misfits / profile_dev).reshape(
        levels, tile_rows, tile_cols
    )
    grad_in = jnp.zeros(w_in.shape, jnp.float32)
    grad_out = jnp.zeros(w_out.shape, jnp.float32)
    for step_index in reversed(range(STEPS)):
        coarse, activity, hidden = history[step_index]
        forcing = ocean * tangent
        forcing_low = forcing.astype(jnp.bfloat16)
        grad_out = grad_out + kernel_grad(hidden, forcing_low)
        derivative = 1.0 - activity * activity
        beside_all = extended_2(forcing, (("lon", 2), ("lat", 1)), 4) * inside_rows(tile_rows, 4)
        spread = conv_valid(beside_all.astype(jnp.bfloat16), back_out)
        margin = (spread * derivative * inside_rows(tile_rows, 2)).astype(jnp.bfloat16)
        sensitivity = margin[:, 2:-2, 2:-2]
        grad_in = grad_in + kernel_grad(coarse, sensitivity)
        tangent = tangent + diffusion * laplace(beside_all, 4) + conv_valid(margin, back_in)
    grad_in, grad_out, square_sum = all_sum((grad_in, grad_out, square_sum), ("lon", "lat"))
    misfit = square_sum / (2.0 * profile_dev * devices * levels)
    return (current, misfit, grad_in, grad_out, tangent * profile_dev)


def solution(mesh):
    placed = (
        P(None, "lat", "lon"),
        P("lat", "lon"),
        P(None, ("lon", "lat")),
        P(("lon", "lat")),
        P(("lon", "lat"), None),
        P(),
        P(),
    )
    return jax.shard_map(
        on_device,
        mesh=mesh,
        in_specs=placed,
        out_specs=(P(None, "lat", "lon"), P(), P(), P(), P(None, "lat", "lon")),
        check_vma=False,
    )
```

```python
import jax
import jax.numpy as jnp
from jax import lax
from jax.experimental import pallas as pl
from jax.experimental.pallas import tpu as pltpu
from jax.sharding import PartitionSpec as P

STEPS = 2
CAP = 32


diffusion = 0.2


def extended_2(cells, sides, width):
    for axis, dim in sides:
        count = lax.axis_size(axis)
        head = lax.slice_in_dim(cells, 0, width, axis=dim)
        tail = lax.slice_in_dim(cells, cells.shape[dim] - width, cells.shape[dim], axis=dim)
        cells = jnp.concatenate(
            [
                lax.ppermute(tail, axis, [(i, (i + 1) % count) for i in range(count)]),
                cells,
                lax.ppermute(head, axis, [((i + 1) % count, i) for i in range(count)]),
            ],
            axis=dim,
        )
    return cells


def laplace(extended, border):
    height = extended.shape[1] - 2 * border
    breadth = extended.shape[2] - 2 * border

    def neighbour(offset_y, offset_x):
        return extended[
            :,
            border + offset_y : border + offset_y + height,
            border + offset_x : border + offset_x + breadth,
        ]

    return (
        neighbour(-1, 0)
        + neighbour(1, 0)
        + neighbour(0, -1)
        + neighbour(0, 1)
        - 4.0 * neighbour(0, 0)
    )


def conv_valid(padded, kernel):
    return lax.conv_general_dilated(
        padded[None],
        kernel,
        (1, 1),
        "VALID",
        dimension_numbers=("NCHW", "OIHW", "NCHW"),
        preferred_element_type=jnp.float32,
    )[0]


def flipped(kernel):
    return jnp.transpose(kernel[:, :, ::-1, ::-1], (1, 0, 2, 3))


def kernel_grad(padded, cotangent):
    return lax.conv_general_dilated(
        padded[None],
        cotangent[None],
        (1, 1),
        "VALID",
        dimension_numbers=("CNHW", "IOHW", "HWNC"),
        preferred_element_type=jnp.float32,
    )


def split3(values):
    high = values.astype(jnp.bfloat16)
    rest = values - high.astype(jnp.float32)
    middle = rest.astype(jnp.bfloat16)
    low = (rest - middle.astype(jnp.float32)).astype(jnp.bfloat16)
    return high, middle, low


def exact_dot(values, onehot):
    high, middle, low = split3(values)
    dims = (((1,), (0,)), ((), ()))
    total = lax.dot_general(high, onehot, dims, preferred_element_type=jnp.float32)
    total = total + lax.dot_general(middle, onehot, dims, preferred_element_type=jnp.float32)
    return total + lax.dot_general(low, onehot, dims, preferred_element_type=jnp.float32)


def pick_columns(values, index, block=512):
    rows, width = values.shape
    count = index.shape[1]

    def body(values_ref, index_ref, out_ref):
        rows_iota = lax.broadcasted_iota(jnp.int32, (width, block), 0)
        onehot = (rows_iota == index_ref[...]).astype(jnp.bfloat16)
        out_ref[...] = exact_dot(values_ref[...], onehot)

    return pl.pallas_call(
        body,
        grid=(count // block,),
        in_specs=[
            pl.BlockSpec((rows, width), lambda i: (0, 0)),
            pl.BlockSpec((1, block), lambda i: (0, i)),
        ],
        out_specs=pl.BlockSpec((rows, block), lambda i: (0, i)),
        out_shape=jax.ShapeDtypeStruct((rows, count), jnp.float32),
        compiler_params=pltpu.CompilerParams(dimension_semantics=("parallel",)),
    )(values, index)


def pick_cells(values, where_to, block=512):
    levels, rows, cols = values.shape
    count = where_to.shape[1]

    def body(values_ref, where_ref, out_ref):
        row_of = where_ref[0:1, :]
        col_of = where_ref[1:2, :]
        cols_iota = lax.broadcasted_iota(jnp.int32, (cols, block), 0)
        onehot = (cols_iota == col_of).astype(jnp.bfloat16)
        total = jnp.zeros((levels, block), jnp.float32)
        for row in range(rows):
            picked = exact_dot(values_ref[:, row, :], onehot)
            total = total + jnp.where(row_of == row, picked, 0.0)
        out_ref[...] = total

    return pl.pallas_call(
        body,
        grid=(count // block,),
        in_specs=[
            pl.BlockSpec((levels, rows, cols), lambda i: (0, 0, 0)),
            pl.BlockSpec((2, block), lambda i: (0, i)),
        ],
        out_specs=pl.BlockSpec((levels, block), lambda i: (0, i)),
        out_shape=jax.ShapeDtypeStruct((levels, count), jnp.float32),
        compiler_params=pltpu.CompilerParams(dimension_semantics=("parallel",)),
    )(values, where_to)


def add_columns(values, index_col, width, block=256):
    rows, count = values.shape

    def body(values_ref, index_ref, out_ref):
        start = pl.program_id(0) * block
        cols_iota = lax.broadcasted_iota(jnp.int32, (count, block), 1) + start
        onehot = (cols_iota == index_ref[...]).astype(jnp.bfloat16)
        out_ref[...] = exact_dot(values_ref[...], onehot)

    return pl.pallas_call(
        body,
        grid=(width // block,),
        in_specs=[
            pl.BlockSpec((rows, count), lambda i: (0, 0)),
            pl.BlockSpec((count, 1), lambda i: (0, 0)),
        ],
        out_specs=pl.BlockSpec((rows, block), lambda i: (0, i)),
        out_shape=jax.ShapeDtypeStruct((rows, width), jnp.float32),
        compiler_params=pltpu.CompilerParams(dimension_semantics=("parallel",)),
    )(values, index_col)


def all_sum(parts, axes):
    count = 1
    for axis in axes:
        count *= lax.axis_size(axis)
    flat = jnp.concatenate([part.reshape(-1) for part in parts])
    size = flat.shape[0]
    chunk = -(-size // count)
    rows = jnp.pad(flat, (0, chunk * count - size)).reshape(count, chunk)
    mine = jnp.sum(lax.all_to_all(rows, axes, 0, 0, tiled=True), axis=0)
    spread = lax.all_to_all(jnp.broadcast_to(mine[None], (count, chunk)), axes, 0, 0, tiled=True)
    flat = spread.reshape(-1)
    sums, offset = [], 0
    for part in parts:
        sums.append(flat[offset : offset + part.size].reshape(part.shape))
        offset += part.size
    return tuple(sums)


def inside_rows(tile_rows, border):
    first_row = lax.axis_index("lat") * tile_rows
    global_rows = first_row + jnp.arange(-border, tile_rows + border, dtype=jnp.int32)
    row_limit = tile_rows * lax.axis_size("lat")
    return ((global_rows >= 0) & (global_rows < row_limit)).astype(jnp.float32)[None, :, None]


def on_device(state, land_mask, observations, profile_cells, profile_counts, w_in, w_out):
    levels, tile_rows, tile_cols = state.shape
    ocean = land_mask.astype(jnp.float32)
    back_in = flipped(w_in)
    back_out = flipped(w_out)
    current = state
    history = []
    for step_index in range(STEPS):
        extended = extended_2(current, (("lon", 2), ("lat", 1)), 4) * inside_rows(tile_rows, 4)
        coarse = extended.astype(jnp.bfloat16)
        activity = jnp.tanh(conv_valid(coarse, w_in))
        hidden = (activity * inside_rows(tile_rows, 2)).astype(jnp.bfloat16)
        closure = conv_valid(hidden, w_out)
        history.append((coarse[:, 2:-2, 2:-2], activity, hidden))
        current = current + ocean * (diffusion * laplace(extended, 4) + closure)
    devices = lax.axis_size("lon") * lax.axis_size("lat")
    profile_dev = observations.shape[1]
    cell_count = tile_rows * tile_cols
    sent_rows = profile_counts[0]
    finish = jnp.cumsum(sent_rows)
    starts = finish - sent_rows
    slot_index = jnp.arange(CAP, dtype=jnp.int32)
    source_row = starts[:, None] + slot_index[None, :]
    filled = (slot_index[None, :] < sent_rows[:, None]).reshape(1, -1)
    picked = jnp.where(filled, source_row.reshape(1, -1), profile_dev)
    source = jnp.concatenate(
        [observations, profile_cells[None, :].astype(jnp.float32)], axis=0
    )
    gathered = pick_columns(source, picked)
    sent_values = gathered[:levels]
    sent_cells = jnp.where(filled, gathered[levels:], float(cell_count))
    payload = jnp.concatenate([sent_values, sent_cells], axis=0)
    arrived = lax.all_to_all(payload, ("lon", "lat"), split_axis=1, concat_axis=1, tiled=True)
    received_values = arrived[:levels]
    received_cells = arrived[levels:].astype(jnp.int32)
    occupied = received_cells < cell_count
    target = jnp.where(occupied, received_cells, cell_count)
    flat_state = current.reshape(levels, cell_count)
    misfits = jnp.where(occupied, jnp.take(flat_state, target[0], axis=1, mode="clip") - received_values, 0.0)
    square_sum = jnp.sum(misfits * misfits)
    tangent = jnp.zeros((levels, cell_count), jnp.float32).at[:, jnp.where(occupied, target, 0)[0]].add(misfits / profile_dev).reshape(
        levels, tile_rows, tile_cols
    )
    grad_in = jnp.zeros(w_in.shape[2:] + w_in.shape[1::-1], jnp.float32)
    grad_out = jnp.zeros(w_out.shape[2:] + w_out.shape[1::-1], jnp.float32)
    for step_index in reversed(range(STEPS)):
        coarse, activity, hidden = history[step_index]
        forcing = ocean * tangent
        forcing_low = forcing.astype(jnp.bfloat16)
        grad_out = grad_out + kernel_grad(hidden, forcing_low)
        derivative = 1.0 - activity * activity
        beside_all = extended_2(forcing, (("lon", 2), ("lat", 1)), 4) * inside_rows(tile_rows, 4)
        spread = conv_valid(beside_all.astype(jnp.bfloat16), back_out)
        margin = (spread * derivative * inside_rows(tile_rows, 2)).astype(jnp.bfloat16)
        sensitivity = margin[:, 2:-2, 2:-2]
        grad_in = grad_in + kernel_grad(coarse, sensitivity)
        tangent = tangent + diffusion * laplace(beside_all, 4) + conv_valid(margin, back_in)
    grad_in, grad_out, square_sum = all_sum((grad_in, grad_out, square_sum), ("lon", "lat"))
    grad_in = jnp.transpose(grad_in, (3, 2, 0, 1))
    grad_out = jnp.transpose(grad_out, (3, 2, 0, 1))
    misfit = square_sum / (2.0 * profile_dev * devices * levels)
    return (current, misfit, grad_in, grad_out, tangent * profile_dev)


def solution(mesh):
    placed = (
        P(None, "lat", "lon"),
        P("lat", "lon"),
        P(None, ("lon", "lat")),
        P(("lon", "lat")),
        P(("lon", "lat"), None),
        P(),
        P(),
    )
    return jax.shard_map(
        on_device,
        mesh=mesh,
        in_specs=placed,
        out_specs=(P(None, "lat", "lon"), P(), P(), P(), P(None, "lat", "lon")),
        check_vma=False,
    )
```

```python
import jax
import jax.numpy as jnp
from jax import lax
from jax.experimental import pallas as pl
from jax.experimental.pallas import tpu as pltpu
from jax.sharding import PartitionSpec as P

STEPS = 2
CAP = 32


diffusion = 0.2


def extended_2(cells, sides, width):
    for axis, dim in sides:
        count = lax.axis_size(axis)
        head = lax.slice_in_dim(cells, 0, width, axis=dim)
        tail = lax.slice_in_dim(cells, cells.shape[dim] - width, cells.shape[dim], axis=dim)
        cells = jnp.concatenate(
            [
                lax.ppermute(tail, axis, [(i, (i + 1) % count) for i in range(count)]),
                cells,
                lax.ppermute(head, axis, [((i + 1) % count, i) for i in range(count)]),
            ],
            axis=dim,
        )
    return cells


def laplace(extended, border):
    height = extended.shape[1] - 2 * border
    breadth = extended.shape[2] - 2 * border

    def neighbour(offset_y, offset_x):
        return extended[
            :,
            border + offset_y : border + offset_y + height,
            border + offset_x : border + offset_x + breadth,
        ]

    return (
        neighbour(-1, 0)
        + neighbour(1, 0)
        + neighbour(0, -1)
        + neighbour(0, 1)
        - 4.0 * neighbour(0, 0)
    )


def conv_valid(padded, kernel):
    return lax.conv_general_dilated(
        padded[None],
        kernel,
        (1, 1),
        "VALID",
        dimension_numbers=("NCHW", "OIHW", "NCHW"),
        preferred_element_type=jnp.float32,
    )[0]


def flipped(kernel):
    return jnp.transpose(kernel[:, :, ::-1, ::-1], (1, 0, 2, 3))


def kernel_grad(padded, cotangent):
    return lax.conv_general_dilated(
        padded[None],
        cotangent[None],
        (1, 1),
        "VALID",
        dimension_numbers=("CNHW", "IOHW", "HWNC"),
        preferred_element_type=jnp.float32,
    )


def split3(values):
    high = values.astype(jnp.bfloat16)
    rest = values - high.astype(jnp.float32)
    middle = rest.astype(jnp.bfloat16)
    low = (rest - middle.astype(jnp.float32)).astype(jnp.bfloat16)
    return high, middle, low


def exact_dot(values, onehot):
    high, middle, low = split3(values)
    dims = (((1,), (0,)), ((), ()))
    total = lax.dot_general(high, onehot, dims, preferred_element_type=jnp.float32)
    total = total + lax.dot_general(middle, onehot, dims, preferred_element_type=jnp.float32)
    return total + lax.dot_general(low, onehot, dims, preferred_element_type=jnp.float32)


def pick_columns(values, index, block=512):
    rows, width = values.shape
    count = index.shape[1]

    def body(values_ref, index_ref, out_ref):
        rows_iota = lax.broadcasted_iota(jnp.int32, (width, block), 0)
        onehot = (rows_iota == index_ref[...]).astype(jnp.bfloat16)
        out_ref[...] = exact_dot(values_ref[...], onehot)

    return pl.pallas_call(
        body,
        grid=(count // block,),
        in_specs=[
            pl.BlockSpec((rows, width), lambda i: (0, 0)),
            pl.BlockSpec((1, block), lambda i: (0, i)),
        ],
        out_specs=pl.BlockSpec((rows, block), lambda i: (0, i)),
        out_shape=jax.ShapeDtypeStruct((rows, count), jnp.float32),
        compiler_params=pltpu.CompilerParams(dimension_semantics=("parallel",)),
    )(values, index)


def pick_cells(values, where_to, block=512):
    levels, rows, cols = values.shape
    count = where_to.shape[1]

    def body(values_ref, where_ref, out_ref):
        row_of = where_ref[0:1, :]
        col_of = where_ref[1:2, :]
        cols_iota = lax.broadcasted_iota(jnp.int32, (cols, block), 0)
        onehot = (cols_iota == col_of).astype(jnp.bfloat16)
        total = jnp.zeros((levels, block), jnp.float32)
        for row in range(rows):
            picked = exact_dot(values_ref[:, row, :], onehot)
            total = total + jnp.where(row_of == row, picked, 0.0)
        out_ref[...] = total

    return pl.pallas_call(
        body,
        grid=(count // block,),
        in_specs=[
            pl.BlockSpec((levels, rows, cols), lambda i: (0, 0, 0)),
            pl.BlockSpec((2, block), lambda i: (0, i)),
        ],
        out_specs=pl.BlockSpec((levels, block), lambda i: (0, i)),
        out_shape=jax.ShapeDtypeStruct((levels, count), jnp.float32),
        compiler_params=pltpu.CompilerParams(dimension_semantics=("parallel",)),
    )(values, where_to)


def add_columns(values, index_col, width, block=256):
    rows, count = values.shape

    def body(values_ref, index_ref, out_ref):
        start = pl.program_id(0) * block
        cols_iota = lax.broadcasted_iota(jnp.int32, (count, block), 1) + start
        onehot = (cols_iota == index_ref[...]).astype(jnp.bfloat16)
        out_ref[...] = exact_dot(values_ref[...], onehot)

    return pl.pallas_call(
        body,
        grid=(width // block,),
        in_specs=[
            pl.BlockSpec((rows, count), lambda i: (0, 0)),
            pl.BlockSpec((count, 1), lambda i: (0, 0)),
        ],
        out_specs=pl.BlockSpec((rows, block), lambda i: (0, i)),
        out_shape=jax.ShapeDtypeStruct((rows, width), jnp.float32),
        compiler_params=pltpu.CompilerParams(dimension_semantics=("parallel",)),
    )(values, index_col)


def all_sum(parts, axes):
    count = 1
    for axis in axes:
        count *= lax.axis_size(axis)
    flat = jnp.concatenate([part.reshape(-1) for part in parts])
    size = flat.shape[0]
    chunk = -(-size // count)
    rows = jnp.pad(flat, (0, chunk * count - size)).reshape(count, chunk)
    mine = jnp.sum(lax.all_to_all(rows, axes, 0, 0, tiled=True), axis=0)
    spread = lax.all_to_all(jnp.broadcast_to(mine[None], (count, chunk)), axes, 0, 0, tiled=True)
    flat = spread.reshape(-1)
    sums, offset = [], 0
    for part in parts:
        sums.append(flat[offset : offset + part.size].reshape(part.shape))
        offset += part.size
    return tuple(sums)


def inside_rows(tile_rows, border):
    first_row = lax.axis_index("lat") * tile_rows
    global_rows = first_row + jnp.arange(-border, tile_rows + border, dtype=jnp.int32)
    row_limit = tile_rows * lax.axis_size("lat")
    return ((global_rows >= 0) & (global_rows < row_limit)).astype(jnp.float32)[None, :, None]


def on_device(state, land_mask, observations, profile_cells, profile_counts, w_in, w_out):
    levels, tile_rows, tile_cols = state.shape
    ocean = land_mask.astype(jnp.float32)
    back_in = flipped(w_in)
    back_out = flipped(w_out)
    current = state
    history = []
    for step_index in range(STEPS):
        extended = extended_2(current, (("lon", 2), ("lat", 1)), 4) * inside_rows(tile_rows, 4)
        coarse = extended.astype(jnp.bfloat16)
        activity = jnp.tanh(conv_valid(coarse, w_in))
        hidden = (activity * inside_rows(tile_rows, 2)).astype(jnp.bfloat16)
        closure = conv_valid(hidden, w_out)
        history.append((coarse[:, 2:-2, 2:-2], activity, hidden))
        current = current + ocean * (diffusion * laplace(extended, 4) + closure)
    devices = lax.axis_size("lon") * lax.axis_size("lat")
    profile_dev = observations.shape[1]
    cell_count = tile_rows * tile_cols
    sent_rows = profile_counts[0]
    finish = jnp.cumsum(sent_rows)
    starts = finish - sent_rows
    slot_index = jnp.arange(CAP, dtype=jnp.int32)
    source_row = starts[:, None] + slot_index[None, :]
    filled = (slot_index[None, :] < sent_rows[:, None]).reshape(1, -1)
    picked = jnp.where(filled, source_row.reshape(1, -1), profile_dev)
    source = jnp.concatenate(
        [observations, profile_cells[None, :].astype(jnp.float32)], axis=0
    )
    gathered = pick_columns(source, picked)
    sent_values = gathered[:levels]
    sent_cells = jnp.where(filled, gathered[levels:], float(cell_count))
    payload = jnp.concatenate([sent_values, sent_cells], axis=0)
    arrived = lax.all_to_all(payload, ("lon", "lat"), split_axis=1, concat_axis=1, tiled=True)
    received_values = arrived[:levels]
    received_cells = arrived[levels:].astype(jnp.int32)
    occupied = received_cells < cell_count
    target = jnp.where(occupied, received_cells, cell_count)
    rows_of_cells = current.reshape(levels, cell_count).T
    slot_cells = jnp.where(occupied, received_cells, 0)[0]
    misfits = jnp.where(
        occupied.T, jnp.take(rows_of_cells, slot_cells, axis=0, mode="clip") - received_values.T, 0.0
    )
    square_sum = jnp.sum(misfits * misfits)
    tangent = (
        jnp.zeros((cell_count, levels), jnp.float32)
        .at[slot_cells]
        .add(misfits / profile_dev)
        .T.reshape(levels, tile_rows, tile_cols)
    )
    grad_in = jnp.zeros(w_in.shape[2:] + w_in.shape[1::-1], jnp.float32)
    grad_out = jnp.zeros(w_out.shape[2:] + w_out.shape[1::-1], jnp.float32)
    for step_index in reversed(range(STEPS)):
        coarse, activity, hidden = history[step_index]
        forcing = ocean * tangent
        forcing_low = forcing.astype(jnp.bfloat16)
        grad_out = grad_out + kernel_grad(hidden, forcing_low)
        derivative = 1.0 - activity * activity
        beside_all = extended_2(forcing, (("lon", 2), ("lat", 1)), 4) * inside_rows(tile_rows, 4)
        spread = conv_valid(beside_all.astype(jnp.bfloat16), back_out)
        margin = (spread * derivative * inside_rows(tile_rows, 2)).astype(jnp.bfloat16)
        sensitivity = margin[:, 2:-2, 2:-2]
        grad_in = grad_in + kernel_grad(coarse, sensitivity)
        tangent = tangent + diffusion * laplace(beside_all, 4) + conv_valid(margin, back_in)
    grad_in, grad_out, square_sum = all_sum((grad_in, grad_out, square_sum), ("lon", "lat"))
    grad_in = jnp.transpose(grad_in, (3, 2, 0, 1))
    grad_out = jnp.transpose(grad_out, (3, 2, 0, 1))
    misfit = square_sum / (2.0 * profile_dev * devices * levels)
    return (current, misfit, grad_in, grad_out, tangent * profile_dev)


def solution(mesh):
    placed = (
        P(None, "lat", "lon"),
        P("lat", "lon"),
        P(None, ("lon", "lat")),
        P(("lon", "lat")),
        P(("lon", "lat"), None),
        P(),
        P(),
    )
    return jax.shard_map(
        on_device,
        mesh=mesh,
        in_specs=placed,
        out_specs=(P(None, "lat", "lon"), P(), P(), P(), P(None, "lat", "lon")),
        check_vma=False,
    )
```

```python
import jax
import jax.numpy as jnp
from jax import lax
from jax.experimental import pallas as pl
from jax.experimental.pallas import tpu as pltpu
from jax.sharding import PartitionSpec as P

STEPS = 2
CAP = 32


diffusion = 0.2


def extended_2(cells, sides, width):
    for axis, dim in sides:
        count = lax.axis_size(axis)
        head = lax.slice_in_dim(cells, 0, width, axis=dim)
        tail = lax.slice_in_dim(cells, cells.shape[dim] - width, cells.shape[dim], axis=dim)
        cells = jnp.concatenate(
            [
                lax.ppermute(tail, axis, [(i, (i + 1) % count) for i in range(count)]),
                cells,
                lax.ppermute(head, axis, [((i + 1) % count, i) for i in range(count)]),
            ],
            axis=dim,
        )
    return cells


def laplace(extended, border):
    height = extended.shape[1] - 2 * border
    breadth = extended.shape[2] - 2 * border

    def neighbour(offset_y, offset_x):
        return extended[
            :,
            border + offset_y : border + offset_y + height,
            border + offset_x : border + offset_x + breadth,
        ]

    return (
        neighbour(-1, 0)
        + neighbour(1, 0)
        + neighbour(0, -1)
        + neighbour(0, 1)
        - 4.0 * neighbour(0, 0)
    )


def conv_valid(padded, kernel):
    return lax.conv_general_dilated(
        padded[None],
        kernel,
        (1, 1),
        "VALID",
        dimension_numbers=("NCHW", "OIHW", "NCHW"),
        preferred_element_type=jnp.float32,
    )[0]


def flipped(kernel):
    return jnp.transpose(kernel[:, :, ::-1, ::-1], (1, 0, 2, 3))


def kernel_grad(padded, cotangent):
    return lax.conv_general_dilated(
        padded[None],
        cotangent[None],
        (1, 1),
        "VALID",
        dimension_numbers=("CNHW", "IOHW", "HWNC"),
        preferred_element_type=jnp.float32,
    )


def split3(values):
    high = values.astype(jnp.bfloat16)
    rest = values - high.astype(jnp.float32)
    middle = rest.astype(jnp.bfloat16)
    low = (rest - middle.astype(jnp.float32)).astype(jnp.bfloat16)
    return high, middle, low


def exact_dot(values, onehot):
    high, middle, low = split3(values)
    dims = (((1,), (0,)), ((), ()))
    total = lax.dot_general(high, onehot, dims, preferred_element_type=jnp.float32)
    total = total + lax.dot_general(middle, onehot, dims, preferred_element_type=jnp.float32)
    return total + lax.dot_general(low, onehot, dims, preferred_element_type=jnp.float32)


def pick_columns(values, index, block=512):
    rows, width = values.shape
    count = index.shape[1]

    def body(values_ref, index_ref, out_ref):
        rows_iota = lax.broadcasted_iota(jnp.int32, (width, block), 0)
        onehot = (rows_iota == index_ref[...]).astype(jnp.bfloat16)
        out_ref[...] = exact_dot(values_ref[...], onehot)

    return pl.pallas_call(
        body,
        grid=(count // block,),
        in_specs=[
            pl.BlockSpec((rows, width), lambda i: (0, 0)),
            pl.BlockSpec((1, block), lambda i: (0, i)),
        ],
        out_specs=pl.BlockSpec((rows, block), lambda i: (0, i)),
        out_shape=jax.ShapeDtypeStruct((rows, count), jnp.float32),
        compiler_params=pltpu.CompilerParams(dimension_semantics=("parallel",)),
    )(values, index)


def pick_cells(values, where_to, block=512):
    levels, rows, cols = values.shape
    count = where_to.shape[1]

    def body(values_ref, where_ref, out_ref):
        row_of = where_ref[0:1, :]
        col_of = where_ref[1:2, :]
        cols_iota = lax.broadcasted_iota(jnp.int32, (cols, block), 0)
        onehot = (cols_iota == col_of).astype(jnp.bfloat16)
        total = jnp.zeros((levels, block), jnp.float32)
        for row in range(rows):
            picked = exact_dot(values_ref[:, row, :], onehot)
            total = total + jnp.where(row_of == row, picked, 0.0)
        out_ref[...] = total

    return pl.pallas_call(
        body,
        grid=(count // block,),
        in_specs=[
            pl.BlockSpec((levels, rows, cols), lambda i: (0, 0, 0)),
            pl.BlockSpec((2, block), lambda i: (0, i)),
        ],
        out_specs=pl.BlockSpec((levels, block), lambda i: (0, i)),
        out_shape=jax.ShapeDtypeStruct((levels, count), jnp.float32),
        compiler_params=pltpu.CompilerParams(dimension_semantics=("parallel",)),
    )(values, where_to)


def add_columns(values, index_col, width, block=256):
    rows, count = values.shape

    def body(values_ref, index_ref, out_ref):
        start = pl.program_id(0) * block
        cols_iota = lax.broadcasted_iota(jnp.int32, (count, block), 1) + start
        onehot = (cols_iota == index_ref[...]).astype(jnp.bfloat16)
        out_ref[...] = exact_dot(values_ref[...], onehot)

    return pl.pallas_call(
        body,
        grid=(width // block,),
        in_specs=[
            pl.BlockSpec((rows, count), lambda i: (0, 0)),
            pl.BlockSpec((count, 1), lambda i: (0, 0)),
        ],
        out_specs=pl.BlockSpec((rows, block), lambda i: (0, i)),
        out_shape=jax.ShapeDtypeStruct((rows, width), jnp.float32),
        compiler_params=pltpu.CompilerParams(dimension_semantics=("parallel",)),
    )(values, index_col)


def all_sum(parts, axes):
    count = 1
    for axis in axes:
        count *= lax.axis_size(axis)
    flat = jnp.concatenate([part.reshape(-1) for part in parts])
    size = flat.shape[0]
    chunk = -(-size // count)
    rows = jnp.pad(flat, (0, chunk * count - size)).reshape(count, chunk)
    mine = jnp.sum(lax.all_to_all(rows, axes, 0, 0, tiled=True), axis=0)
    spread = lax.all_to_all(jnp.broadcast_to(mine[None], (count, chunk)), axes, 0, 0, tiled=True)
    flat = spread.reshape(-1)
    sums, offset = [], 0
    for part in parts:
        sums.append(flat[offset : offset + part.size].reshape(part.shape))
        offset += part.size
    return tuple(sums)


def inside_rows(tile_rows, border):
    first_row = lax.axis_index("lat") * tile_rows
    global_rows = first_row + jnp.arange(-border, tile_rows + border, dtype=jnp.int32)
    row_limit = tile_rows * lax.axis_size("lat")
    return ((global_rows >= 0) & (global_rows < row_limit)).astype(jnp.float32)[None, :, None]


def on_device(state, land_mask, observations, profile_cells, profile_counts, w_in, w_out):
    levels, tile_rows, tile_cols = state.shape
    ocean = land_mask.astype(jnp.float32)
    back_in = flipped(w_in)
    back_out = flipped(w_out)
    current = state
    history = []
    for step_index in range(STEPS):
        extended = extended_2(current, (("lon", 2), ("lat", 1)), 4) * inside_rows(tile_rows, 4)
        coarse = extended.astype(jnp.bfloat16)
        activity = jnp.tanh(conv_valid(coarse, w_in))
        hidden = (activity * inside_rows(tile_rows, 2)).astype(jnp.bfloat16)
        closure = conv_valid(hidden, w_out)
        history.append((coarse[:, 2:-2, 2:-2], activity, hidden))
        current = current + ocean * (diffusion * laplace(extended, 4) + closure)
    devices = lax.axis_size("lon") * lax.axis_size("lat")
    profile_dev = observations.shape[1]
    cell_count = tile_rows * tile_cols
    sent_rows = profile_counts[0]
    finish = jnp.cumsum(sent_rows)
    starts = finish - sent_rows
    slot_index = jnp.arange(CAP, dtype=jnp.int32)
    source_row = starts[:, None] + slot_index[None, :]
    filled = (slot_index[None, :] < sent_rows[:, None]).reshape(1, -1)
    picked = jnp.where(filled, source_row.reshape(1, -1), profile_dev)
    source = jnp.concatenate(
        [observations, profile_cells[None, :].astype(jnp.float32)], axis=0
    )
    gathered = pick_columns(source, picked)
    sent_values = gathered[:levels]
    sent_cells = jnp.where(filled, gathered[levels:], float(cell_count))
    payload = jnp.concatenate([sent_values, sent_cells], axis=0)
    arrived = lax.all_to_all(payload, ("lon", "lat"), split_axis=1, concat_axis=1, tiled=True)
    received_values = arrived[:levels]
    received_cells = arrived[levels:].astype(jnp.int32)
    occupied = received_cells < cell_count
    target = jnp.where(occupied, received_cells, cell_count)
    row_of = jnp.where(occupied, received_cells // tile_cols, tile_rows)[0]
    col_of = (received_cells % tile_cols)[0]
    row_hit = row_of[None, :] == jnp.arange(tile_rows, dtype=jnp.int32)[:, None]
    col_hit = col_of[:, None] == jnp.arange(tile_cols, dtype=jnp.int32)[None, :]
    col_onehot = col_hit.astype(jnp.bfloat16)
    by_cols = exact_dot(current.reshape(levels * tile_rows, tile_cols), col_onehot.T)
    picked = jnp.sum(
        jnp.where(row_hit[None], by_cols.reshape(levels, tile_rows, -1), 0.0), axis=1
    )
    misfits = jnp.where(occupied, picked - received_values, 0.0)
    square_sum = jnp.sum(misfits * misfits)
    tangent = jnp.zeros((levels * tile_rows, tile_cols), jnp.float32)
    for part in split3(misfits / profile_dev):
        spread_rows = jnp.where(row_hit[None], part[:, None, :], jnp.zeros((), jnp.bfloat16))
        tangent = tangent + jnp.dot(
            spread_rows.reshape(levels * tile_rows, -1), col_onehot, preferred_element_type=jnp.float32
        )
    tangent = tangent.reshape(levels, tile_rows, tile_cols)
    grad_in = jnp.zeros(w_in.shape[2:] + w_in.shape[1::-1], jnp.float32)
    grad_out = jnp.zeros(w_out.shape[2:] + w_out.shape[1::-1], jnp.float32)
    for step_index in reversed(range(STEPS)):
        coarse, activity, hidden = history[step_index]
        forcing = ocean * tangent
        forcing_low = forcing.astype(jnp.bfloat16)
        grad_out = grad_out + kernel_grad(hidden, forcing_low)
        derivative = 1.0 - activity * activity
        beside_all = extended_2(forcing, (("lon", 2), ("lat", 1)), 4) * inside_rows(tile_rows, 4)
        spread = conv_valid(beside_all.astype(jnp.bfloat16), back_out)
        margin = (spread * derivative * inside_rows(tile_rows, 2)).astype(jnp.bfloat16)
        sensitivity = margin[:, 2:-2, 2:-2]
        grad_in = grad_in + kernel_grad(coarse, sensitivity)
        tangent = tangent + diffusion * laplace(beside_all, 4) + conv_valid(margin, back_in)
    grad_in, grad_out, square_sum = all_sum((grad_in, grad_out, square_sum), ("lon", "lat"))
    grad_in = jnp.transpose(grad_in, (3, 2, 0, 1))
    grad_out = jnp.transpose(grad_out, (3, 2, 0, 1))
    misfit = square_sum / (2.0 * profile_dev * devices * levels)
    return (current, misfit, grad_in, grad_out, tangent * profile_dev)


def solution(mesh):
    placed = (
        P(None, "lat", "lon"),
        P("lat", "lon"),
        P(None, ("lon", "lat")),
        P(("lon", "lat")),
        P(("lon", "lat"), None),
        P(),
        P(),
    )
    return jax.shard_map(
        on_device,
        mesh=mesh,
        in_specs=placed,
        out_specs=(P(None, "lat", "lon"), P(), P(), P(), P(None, "lat", "lon")),
        check_vma=False,
    )
```

```python
import jax
import jax.numpy as jnp
from jax import lax
from jax.experimental import pallas as pl
from jax.experimental.pallas import tpu as pltpu
from jax.sharding import PartitionSpec as P

STEPS = 2
CAP = 32


diffusion = 0.2


def extended_2(cells, sides, width):
    for axis, dim in sides:
        count = lax.axis_size(axis)
        head = lax.slice_in_dim(cells, 0, width, axis=dim)
        tail = lax.slice_in_dim(cells, cells.shape[dim] - width, cells.shape[dim], axis=dim)
        cells = jnp.concatenate(
            [
                lax.ppermute(tail, axis, [(i, (i + 1) % count) for i in range(count)]),
                cells,
                lax.ppermute(head, axis, [((i + 1) % count, i) for i in range(count)]),
            ],
            axis=dim,
        )
    return cells


def laplace(extended, border):
    height = extended.shape[1] - 2 * border
    breadth = extended.shape[2] - 2 * border

    def neighbour(offset_y, offset_x):
        return extended[
            :,
            border + offset_y : border + offset_y + height,
            border + offset_x : border + offset_x + breadth,
        ]

    return (
        neighbour(-1, 0)
        + neighbour(1, 0)
        + neighbour(0, -1)
        + neighbour(0, 1)
        - 4.0 * neighbour(0, 0)
    )


def conv_valid(padded, kernel):
    return lax.conv_general_dilated(
        padded[None],
        kernel,
        (1, 1),
        "VALID",
        dimension_numbers=("NCHW", "OIHW", "NCHW"),
        preferred_element_type=jnp.float32,
    )[0]


def flipped(kernel):
    return jnp.transpose(kernel[:, :, ::-1, ::-1], (1, 0, 2, 3))


def kernel_grad(padded, cotangent):
    return lax.conv_general_dilated(
        padded[None],
        cotangent[None],
        (1, 1),
        "VALID",
        dimension_numbers=("CNHW", "IOHW", "HWNC"),
        preferred_element_type=jnp.float32,
    )


def split3(values):
    high = lax.reduce_precision(values, exponent_bits=8, mantissa_bits=7)
    rest = values - high
    middle = lax.reduce_precision(rest, exponent_bits=8, mantissa_bits=7)
    low = rest - middle
    return high.astype(jnp.bfloat16), middle.astype(jnp.bfloat16), low.astype(jnp.bfloat16)


def exact_dot(values, onehot):
    high, middle, low = split3(values)
    dims = (((1,), (0,)), ((), ()))
    total = lax.dot_general(high, onehot, dims, preferred_element_type=jnp.float32)
    total = total + lax.dot_general(middle, onehot, dims, preferred_element_type=jnp.float32)
    return total + lax.dot_general(low, onehot, dims, preferred_element_type=jnp.float32)


def pick_columns(values, index, block=512):
    rows, width = values.shape
    count = index.shape[1]

    def body(values_ref, index_ref, out_ref):
        rows_iota = lax.broadcasted_iota(jnp.int32, (width, block), 0)
        onehot = (rows_iota == index_ref[...]).astype(jnp.bfloat16)
        out_ref[...] = exact_dot(values_ref[...], onehot)

    return pl.pallas_call(
        body,
        grid=(count // block,),
        in_specs=[
            pl.BlockSpec((rows, width), lambda i: (0, 0)),
            pl.BlockSpec((1, block), lambda i: (0, i)),
        ],
        out_specs=pl.BlockSpec((rows, block), lambda i: (0, i)),
        out_shape=jax.ShapeDtypeStruct((rows, count), jnp.float32),
        compiler_params=pltpu.CompilerParams(dimension_semantics=("parallel",)),
    )(values, index)


def pick_cells(values, where_to, block=512):
    levels, rows, cols = values.shape
    count = where_to.shape[1]

    def body(values_ref, where_ref, out_ref):
        row_of = where_ref[0:1, :]
        col_of = where_ref[1:2, :]
        cols_iota = lax.broadcasted_iota(jnp.int32, (cols, block), 0)
        onehot = (cols_iota == col_of).astype(jnp.bfloat16)
        total = jnp.zeros((levels, block), jnp.float32)
        for row in range(rows):
            picked = exact_dot(values_ref[:, row, :], onehot)
            total = total + jnp.where(row_of == row, picked, 0.0)
        out_ref[...] = total

    return pl.pallas_call(
        body,
        grid=(count // block,),
        in_specs=[
            pl.BlockSpec((levels, rows, cols), lambda i: (0, 0, 0)),
            pl.BlockSpec((2, block), lambda i: (0, i)),
        ],
        out_specs=pl.BlockSpec((levels, block), lambda i: (0, i)),
        out_shape=jax.ShapeDtypeStruct((levels, count), jnp.float32),
        compiler_params=pltpu.CompilerParams(dimension_semantics=("parallel",)),
    )(values, where_to)


def add_columns(values, index_col, width, block=256):
    rows, count = values.shape

    def body(values_ref, index_ref, out_ref):
        start = pl.program_id(0) * block
        cols_iota = lax.broadcasted_iota(jnp.int32, (count, block), 1) + start
        onehot = (cols_iota == index_ref[...]).astype(jnp.bfloat16)
        out_ref[...] = exact_dot(values_ref[...], onehot)

    return pl.pallas_call(
        body,
        grid=(width // block,),
        in_specs=[
            pl.BlockSpec((rows, count), lambda i: (0, 0)),
            pl.BlockSpec((count, 1), lambda i: (0, 0)),
        ],
        out_specs=pl.BlockSpec((rows, block), lambda i: (0, i)),
        out_shape=jax.ShapeDtypeStruct((rows, width), jnp.float32),
        compiler_params=pltpu.CompilerParams(dimension_semantics=("parallel",)),
    )(values, index_col)


def all_sum(parts, axes):
    count = 1
    for axis in axes:
        count *= lax.axis_size(axis)
    flat = jnp.concatenate([part.reshape(-1) for part in parts])
    size = flat.shape[0]
    chunk = -(-size // count)
    rows = jnp.pad(flat, (0, chunk * count - size)).reshape(count, chunk)
    mine = jnp.sum(lax.all_to_all(rows, axes, 0, 0, tiled=True), axis=0)
    spread = lax.all_to_all(jnp.broadcast_to(mine[None], (count, chunk)), axes, 0, 0, tiled=True)
    flat = spread.reshape(-1)
    sums, offset = [], 0
    for part in parts:
        sums.append(flat[offset : offset + part.size].reshape(part.shape))
        offset += part.size
    return tuple(sums)


def inside_rows(tile_rows, border):
    first_row = lax.axis_index("lat") * tile_rows
    global_rows = first_row + jnp.arange(-border, tile_rows + border, dtype=jnp.int32)
    row_limit = tile_rows * lax.axis_size("lat")
    return ((global_rows >= 0) & (global_rows < row_limit)).astype(jnp.float32)[None, :, None]


def on_device(state, land_mask, observations, profile_cells, profile_counts, w_in, w_out):
    levels, tile_rows, tile_cols = state.shape
    ocean = land_mask.astype(jnp.float32)
    back_in = flipped(w_in)
    back_out = flipped(w_out)
    current = state
    history = []
    for step_index in range(STEPS):
        extended = extended_2(current, (("lon", 2), ("lat", 1)), 4) * inside_rows(tile_rows, 4)
        coarse = extended.astype(jnp.bfloat16)
        activity = jnp.tanh(conv_valid(coarse, w_in))
        hidden = (activity * inside_rows(tile_rows, 2)).astype(jnp.bfloat16)
        closure = conv_valid(hidden, w_out)
        history.append((coarse[:, 2:-2, 2:-2], activity, hidden))
        current = current + ocean * (diffusion * laplace(extended, 4) + closure)
    devices = lax.axis_size("lon") * lax.axis_size("lat")
    profile_dev = observations.shape[1]
    cell_count = tile_rows * tile_cols
    sent_rows = profile_counts[0]
    finish = jnp.cumsum(sent_rows)
    starts = finish - sent_rows
    slot_index = jnp.arange(CAP, dtype=jnp.int32)
    source_row = starts[:, None] + slot_index[None, :]
    filled = (slot_index[None, :] < sent_rows[:, None]).reshape(1, -1)
    picked = jnp.where(filled, source_row.reshape(1, -1), profile_dev)
    source = jnp.concatenate(
        [observations, profile_cells[None, :].astype(jnp.float32)], axis=0
    )
    gathered = pick_columns(source, picked)
    sent_values = gathered[:levels]
    sent_cells = jnp.where(filled, gathered[levels:], float(cell_count))
    payload = jnp.concatenate([sent_values, sent_cells], axis=0)
    arrived = lax.all_to_all(payload, ("lon", "lat"), split_axis=1, concat_axis=1, tiled=True)
    received_values = arrived[:levels]
    received_cells = arrived[levels:].astype(jnp.int32)
    occupied = received_cells < cell_count
    target = jnp.where(occupied, received_cells, cell_count)
    row_of = jnp.where(occupied, received_cells // tile_cols, tile_rows)[0]
    col_of = (received_cells % tile_cols)[0]
    row_hit = row_of[None, :] == jnp.arange(tile_rows, dtype=jnp.int32)[:, None]
    col_hit = col_of[:, None] == jnp.arange(tile_cols, dtype=jnp.int32)[None, :]
    col_onehot = col_hit.astype(jnp.bfloat16)
    by_cols = exact_dot(current.reshape(levels * tile_rows, tile_cols), col_onehot.T)
    picked = jnp.sum(
        jnp.where(row_hit[None], by_cols.reshape(levels, tile_rows, -1), 0.0), axis=1
    )
    misfits = jnp.where(occupied, picked - received_values, 0.0)
    square_sum = jnp.sum(misfits * misfits)
    tangent = jnp.zeros((levels * tile_rows, tile_cols), jnp.float32)
    for part in split3(misfits / profile_dev):
        spread_rows = jnp.where(row_hit[None], part[:, None, :], jnp.zeros((), jnp.bfloat16))
        tangent = tangent + jnp.dot(
            spread_rows.reshape(levels * tile_rows, -1), col_onehot, preferred_element_type=jnp.float32
        )
    tangent = tangent.reshape(levels, tile_rows, tile_cols)
    grad_in = jnp.zeros(w_in.shape[2:] + w_in.shape[1::-1], jnp.float32)
    grad_out = jnp.zeros(w_out.shape[2:] + w_out.shape[1::-1], jnp.float32)
    for step_index in reversed(range(STEPS)):
        coarse, activity, hidden = history[step_index]
        forcing = ocean * tangent
        forcing_low = forcing.astype(jnp.bfloat16)
        grad_out = grad_out + kernel_grad(hidden, forcing_low)
        derivative = 1.0 - activity * activity
        beside_all = extended_2(forcing, (("lon", 2), ("lat", 1)), 4) * inside_rows(tile_rows, 4)
        spread = conv_valid(beside_all.astype(jnp.bfloat16), back_out)
        margin = (spread * derivative * inside_rows(tile_rows, 2)).astype(jnp.bfloat16)
        sensitivity = margin[:, 2:-2, 2:-2]
        grad_in = grad_in + kernel_grad(coarse, sensitivity)
        tangent = tangent + diffusion * laplace(beside_all, 4) + conv_valid(margin, back_in)
    grad_in, grad_out, square_sum = all_sum((grad_in, grad_out, square_sum), ("lon", "lat"))
    grad_in = jnp.transpose(grad_in, (3, 2, 0, 1))
    grad_out = jnp.transpose(grad_out, (3, 2, 0, 1))
    misfit = square_sum / (2.0 * profile_dev * devices * levels)
    return (current, misfit, grad_in, grad_out, tangent * profile_dev)


def solution(mesh):
    placed = (
        P(None, "lat", "lon"),
        P("lat", "lon"),
        P(None, ("lon", "lat")),
        P(("lon", "lat")),
        P(("lon", "lat"), None),
        P(),
        P(),
    )
    return jax.shard_map(
        on_device,
        mesh=mesh,
        in_specs=placed,
        out_specs=(P(None, "lat", "lon"), P(), P(), P(), P(None, "lat", "lon")),
        check_vma=False,
    )
```

```python
import jax
import jax.numpy as jnp
from jax import lax
from jax.experimental import pallas as pl
from jax.experimental.pallas import tpu as pltpu
from jax.sharding import PartitionSpec as P

STEPS = 2
CAP = 32


diffusion = 0.2


def extended_2(cells, sides, width):
    for axis, dim in sides:
        count = lax.axis_size(axis)
        head = lax.slice_in_dim(cells, 0, width, axis=dim)
        tail = lax.slice_in_dim(cells, cells.shape[dim] - width, cells.shape[dim], axis=dim)
        cells = jnp.concatenate(
            [
                lax.ppermute(tail, axis, [(i, (i + 1) % count) for i in range(count)]),
                cells,
                lax.ppermute(head, axis, [((i + 1) % count, i) for i in range(count)]),
            ],
            axis=dim,
        )
    return cells


def laplace(extended, border):
    height = extended.shape[1] - 2 * border
    breadth = extended.shape[2] - 2 * border

    def neighbour(offset_y, offset_x):
        return extended[
            :,
            border + offset_y : border + offset_y + height,
            border + offset_x : border + offset_x + breadth,
        ]

    return (
        neighbour(-1, 0)
        + neighbour(1, 0)
        + neighbour(0, -1)
        + neighbour(0, 1)
        - 4.0 * neighbour(0, 0)
    )


def conv_valid(padded, kernel):
    return lax.conv_general_dilated(
        padded[None],
        kernel,
        (1, 1),
        "VALID",
        dimension_numbers=("NCHW", "OIHW", "NCHW"),
        preferred_element_type=jnp.float32,
    )[0]


def flipped(kernel):
    return jnp.transpose(kernel[:, :, ::-1, ::-1], (1, 0, 2, 3))


def kernel_grad(padded, cotangent):
    return lax.conv_general_dilated(
        padded[None],
        cotangent[None],
        (1, 1),
        "VALID",
        dimension_numbers=("CNHW", "IOHW", "HWNC"),
        preferred_element_type=jnp.float32,
    )


def split3(values):
    high = lax.reduce_precision(values, exponent_bits=8, mantissa_bits=7)
    rest = values - high
    middle = lax.reduce_precision(rest, exponent_bits=8, mantissa_bits=7)
    low = rest - middle
    return high.astype(jnp.bfloat16), middle.astype(jnp.bfloat16), low.astype(jnp.bfloat16)


def exact_dot(values, onehot):
    high, middle, low = split3(values)
    dims = (((1,), (0,)), ((), ()))
    total = lax.dot_general(high, onehot, dims, preferred_element_type=jnp.float32)
    total = total + lax.dot_general(middle, onehot, dims, preferred_element_type=jnp.float32)
    return total + lax.dot_general(low, onehot, dims, preferred_element_type=jnp.float32)


def pick_columns(values, index, block=512):
    rows, width = values.shape
    count = index.shape[1]

    def body(values_ref, index_ref, out_ref):
        rows_iota = lax.broadcasted_iota(jnp.int32, (width, block), 0)
        onehot = (rows_iota == index_ref[...]).astype(jnp.bfloat16)
        out_ref[...] = exact_dot(values_ref[...], onehot)

    return pl.pallas_call(
        body,
        grid=(count // block,),
        in_specs=[
            pl.BlockSpec((rows, width), lambda i: (0, 0)),
            pl.BlockSpec((1, block), lambda i: (0, i)),
        ],
        out_specs=pl.BlockSpec((rows, block), lambda i: (0, i)),
        out_shape=jax.ShapeDtypeStruct((rows, count), jnp.float32),
        compiler_params=pltpu.CompilerParams(dimension_semantics=("parallel",)),
    )(values, index)


def pick_cells(values, where_to, block=512):
    levels, rows, cols = values.shape
    count = where_to.shape[1]

    def body(values_ref, where_ref, out_ref):
        row_of = where_ref[0:1, :]
        col_of = where_ref[1:2, :]
        cols_iota = lax.broadcasted_iota(jnp.int32, (cols, block), 0)
        onehot = (cols_iota == col_of).astype(jnp.bfloat16)
        total = jnp.zeros((levels, block), jnp.float32)
        for row in range(rows):
            picked = exact_dot(values_ref[:, row, :], onehot)
            total = total + jnp.where(row_of == row, picked, 0.0)
        out_ref[...] = total

    return pl.pallas_call(
        body,
        grid=(count // block,),
        in_specs=[
            pl.BlockSpec((levels, rows, cols), lambda i: (0, 0, 0)),
            pl.BlockSpec((2, block), lambda i: (0, i)),
        ],
        out_specs=pl.BlockSpec((levels, block), lambda i: (0, i)),
        out_shape=jax.ShapeDtypeStruct((levels, count), jnp.float32),
        compiler_params=pltpu.CompilerParams(dimension_semantics=("parallel",)),
    )(values, where_to)


def add_columns(values, index_col, width, block=256):
    rows, count = values.shape

    def body(values_ref, index_ref, out_ref):
        start = pl.program_id(0) * block
        cols_iota = lax.broadcasted_iota(jnp.int32, (count, block), 1) + start
        onehot = (cols_iota == index_ref[...]).astype(jnp.bfloat16)
        out_ref[...] = exact_dot(values_ref[...], onehot)

    return pl.pallas_call(
        body,
        grid=(width // block,),
        in_specs=[
            pl.BlockSpec((rows, count), lambda i: (0, 0)),
            pl.BlockSpec((count, 1), lambda i: (0, 0)),
        ],
        out_specs=pl.BlockSpec((rows, block), lambda i: (0, i)),
        out_shape=jax.ShapeDtypeStruct((rows, width), jnp.float32),
        compiler_params=pltpu.CompilerParams(dimension_semantics=("parallel",)),
    )(values, index_col)


def all_sum(parts, axes):
    count = 1
    for axis in axes:
        count *= lax.axis_size(axis)
    flat = jnp.concatenate([part.reshape(-1) for part in parts])
    size = flat.shape[0]
    chunk = -(-size // count)
    rows = jnp.pad(flat, (0, chunk * count - size)).reshape(count, chunk)
    mine = jnp.sum(lax.all_to_all(rows, axes, 0, 0, tiled=True), axis=0)
    spread = lax.all_to_all(jnp.broadcast_to(mine[None], (count, chunk)), axes, 0, 0, tiled=True)
    flat = spread.reshape(-1)
    sums, offset = [], 0
    for part in parts:
        sums.append(flat[offset : offset + part.size].reshape(part.shape))
        offset += part.size
    return tuple(sums)


def inside_rows(tile_rows, border):
    first_row = lax.axis_index("lat") * tile_rows
    global_rows = first_row + jnp.arange(-border, tile_rows + border, dtype=jnp.int32)
    row_limit = tile_rows * lax.axis_size("lat")
    return ((global_rows >= 0) & (global_rows < row_limit)).astype(jnp.float32)[None, :, None]


def on_device(state, land_mask, observations, profile_cells, profile_counts, w_in, w_out):
    levels, tile_rows, tile_cols = state.shape
    ocean = land_mask.astype(jnp.float32)
    back_in = flipped(w_in)
    back_out = flipped(w_out)
    current = state
    history = []
    both = extended_2(
        jnp.concatenate([current, ocean[None]], axis=0), (("lon", 2), ("lat", 1)), 8
    ) * inside_rows(tile_rows, 8)
    wide, ocean_wide = both[:levels], both[levels]
    coarse_wide = wide.astype(jnp.bfloat16)
    activity_wide = jnp.tanh(conv_valid(coarse_wide, w_in))
    hidden_wide = (activity_wide * inside_rows(tile_rows, 6)).astype(jnp.bfloat16)
    closure_wide = conv_valid(hidden_wide, w_out)
    history.append(
        (coarse_wide[:, 6:-6, 6:-6], activity_wide[:, 4:-4, 4:-4], hidden_wide[:, 4:-4, 4:-4])
    )
    extended = (
        wide[:, 4:-4, 4:-4]
        + ocean_wide[None, 4:-4, 4:-4] * (diffusion * laplace(wide, 4) + closure_wide)
    ) * inside_rows(tile_rows, 4)
    current = extended[:, 4:-4, 4:-4]
    for step_index in range(1, STEPS):
        coarse = extended.astype(jnp.bfloat16)
        activity = jnp.tanh(conv_valid(coarse, w_in))
        hidden = (activity * inside_rows(tile_rows, 2)).astype(jnp.bfloat16)
        closure = conv_valid(hidden, w_out)
        history.append((coarse[:, 2:-2, 2:-2], activity, hidden))
        current = current + ocean * (diffusion * laplace(extended, 4) + closure)
    devices = lax.axis_size("lon") * lax.axis_size("lat")
    profile_dev = observations.shape[1]
    cell_count = tile_rows * tile_cols
    sent_rows = profile_counts[0]
    finish = jnp.cumsum(sent_rows)
    starts = finish - sent_rows
    slot_index = jnp.arange(CAP, dtype=jnp.int32)
    source_row = starts[:, None] + slot_index[None, :]
    filled = (slot_index[None, :] < sent_rows[:, None]).reshape(1, -1)
    picked = jnp.where(filled, source_row.reshape(1, -1), profile_dev)
    source = jnp.concatenate(
        [observations, profile_cells[None, :].astype(jnp.float32)], axis=0
    )
    gathered = pick_columns(source, picked)
    sent_values = gathered[:levels]
    sent_cells = jnp.where(filled, gathered[levels:], float(cell_count))
    payload = jnp.concatenate([sent_values, sent_cells], axis=0)
    arrived = lax.all_to_all(payload, ("lon", "lat"), split_axis=1, concat_axis=1, tiled=True)
    received_values = arrived[:levels]
    received_cells = arrived[levels:].astype(jnp.int32)
    occupied = received_cells < cell_count
    target = jnp.where(occupied, received_cells, cell_count)
    row_of = jnp.where(occupied, received_cells // tile_cols, tile_rows)[0]
    col_of = (received_cells % tile_cols)[0]
    row_hit = row_of[None, :] == jnp.arange(tile_rows, dtype=jnp.int32)[:, None]
    col_hit = col_of[:, None] == jnp.arange(tile_cols, dtype=jnp.int32)[None, :]
    col_onehot = col_hit.astype(jnp.bfloat16)
    by_cols = exact_dot(current.reshape(levels * tile_rows, tile_cols), col_onehot.T)
    picked = jnp.sum(
        jnp.where(row_hit[None], by_cols.reshape(levels, tile_rows, -1), 0.0), axis=1
    )
    misfits = jnp.where(occupied, picked - received_values, 0.0)
    square_sum = jnp.sum(misfits * misfits)
    tangent = jnp.zeros((levels * tile_rows, tile_cols), jnp.float32)
    for part in split3(misfits / profile_dev):
        spread_rows = jnp.where(row_hit[None], part[:, None, :], jnp.zeros((), jnp.bfloat16))
        tangent = tangent + jnp.dot(
            spread_rows.reshape(levels * tile_rows, -1), col_onehot, preferred_element_type=jnp.float32
        )
    tangent = tangent.reshape(levels, tile_rows, tile_cols)
    grad_in = jnp.zeros(w_in.shape[2:] + w_in.shape[1::-1], jnp.float32)
    grad_out = jnp.zeros(w_out.shape[2:] + w_out.shape[1::-1], jnp.float32)
    for step_index in reversed(range(STEPS)):
        coarse, activity, hidden = history[step_index]
        forcing = ocean * tangent
        forcing_low = forcing.astype(jnp.bfloat16)
        grad_out = grad_out + kernel_grad(hidden, forcing_low)
        derivative = 1.0 - activity * activity
        beside_all = extended_2(forcing, (("lon", 2), ("lat", 1)), 4) * inside_rows(tile_rows, 4)
        spread = conv_valid(beside_all.astype(jnp.bfloat16), back_out)
        margin = (spread * derivative * inside_rows(tile_rows, 2)).astype(jnp.bfloat16)
        sensitivity = margin[:, 2:-2, 2:-2]
        grad_in = grad_in + kernel_grad(coarse, sensitivity)
        tangent = tangent + diffusion * laplace(beside_all, 4) + conv_valid(margin, back_in)
    grad_in, grad_out, square_sum = all_sum((grad_in, grad_out, square_sum), ("lon", "lat"))
    grad_in = jnp.transpose(grad_in, (3, 2, 0, 1))
    grad_out = jnp.transpose(grad_out, (3, 2, 0, 1))
    misfit = square_sum / (2.0 * profile_dev * devices * levels)
    return (current, misfit, grad_in, grad_out, tangent * profile_dev)


def solution(mesh):
    placed = (
        P(None, "lat", "lon"),
        P("lat", "lon"),
        P(None, ("lon", "lat")),
        P(("lon", "lat")),
        P(("lon", "lat"), None),
        P(),
        P(),
    )
    return jax.shard_map(
        on_device,
        mesh=mesh,
        in_specs=placed,
        out_specs=(P(None, "lat", "lon"), P(), P(), P(), P(None, "lat", "lon")),
        check_vma=False,
    )
```

```python
import jax
import jax.numpy as jnp
from jax import lax
from jax.experimental import pallas as pl
from jax.experimental.pallas import tpu as pltpu
from jax.sharding import PartitionSpec as P

STEPS = 2
CAP = 32


diffusion = 0.2


def extended_2(cells, sides, width):
    for axis, dim in sides:
        count = lax.axis_size(axis)
        head = lax.slice_in_dim(cells, 0, width, axis=dim)
        tail = lax.slice_in_dim(cells, cells.shape[dim] - width, cells.shape[dim], axis=dim)
        cells = jnp.concatenate(
            [
                lax.ppermute(tail, axis, [(i, (i + 1) % count) for i in range(count)]),
                cells,
                lax.ppermute(head, axis, [((i + 1) % count, i) for i in range(count)]),
            ],
            axis=dim,
        )
    return cells


def laplace(extended, border):
    height = extended.shape[1] - 2 * border
    breadth = extended.shape[2] - 2 * border

    def neighbour(offset_y, offset_x):
        return extended[
            :,
            border + offset_y : border + offset_y + height,
            border + offset_x : border + offset_x + breadth,
        ]

    return (
        neighbour(-1, 0)
        + neighbour(1, 0)
        + neighbour(0, -1)
        + neighbour(0, 1)
        - 4.0 * neighbour(0, 0)
    )


def conv_valid(padded, kernel):
    return lax.conv_general_dilated(
        padded[None],
        kernel,
        (1, 1),
        "VALID",
        dimension_numbers=("NCHW", "OIHW", "NCHW"),
        preferred_element_type=jnp.float32,
    )[0]


def flipped(kernel):
    return jnp.transpose(kernel[:, :, ::-1, ::-1], (1, 0, 2, 3))


def kernel_grad(padded, cotangent):
    return lax.conv_general_dilated(
        padded[None],
        cotangent[None],
        (1, 1),
        "VALID",
        dimension_numbers=("CNHW", "IOHW", "HWNC"),
        preferred_element_type=jnp.float32,
    )


def split3(values):
    high = lax.reduce_precision(values, exponent_bits=8, mantissa_bits=7)
    rest = values - high
    middle = lax.reduce_precision(rest, exponent_bits=8, mantissa_bits=7)
    low = rest - middle
    return high.astype(jnp.bfloat16), middle.astype(jnp.bfloat16), low.astype(jnp.bfloat16)


def exact_dot(values, onehot):
    high, middle, low = split3(values)
    dims = (((1,), (0,)), ((), ()))
    total = lax.dot_general(high, onehot, dims, preferred_element_type=jnp.float32)
    total = total + lax.dot_general(middle, onehot, dims, preferred_element_type=jnp.float32)
    return total + lax.dot_general(low, onehot, dims, preferred_element_type=jnp.float32)


def pick_columns(values, index, block=512):
    rows, width = values.shape
    count = index.shape[1]

    def body(values_ref, index_ref, out_ref):
        rows_iota = lax.broadcasted_iota(jnp.int32, (width, block), 0)
        onehot = (rows_iota == index_ref[...]).astype(jnp.bfloat16)
        out_ref[...] = exact_dot(values_ref[...], onehot)

    return pl.pallas_call(
        body,
        grid=(count // block,),
        in_specs=[
            pl.BlockSpec((rows, width), lambda i: (0, 0)),
            pl.BlockSpec((1, block), lambda i: (0, i)),
        ],
        out_specs=pl.BlockSpec((rows, block), lambda i: (0, i)),
        out_shape=jax.ShapeDtypeStruct((rows, count), jnp.float32),
        compiler_params=pltpu.CompilerParams(dimension_semantics=("parallel",)),
    )(values, index)


def pick_cells(values, where_to, block=512):
    levels, rows, cols = values.shape
    count = where_to.shape[1]

    def body(values_ref, where_ref, out_ref):
        row_of = where_ref[0:1, :]
        col_of = where_ref[1:2, :]
        cols_iota = lax.broadcasted_iota(jnp.int32, (cols, block), 0)
        onehot = (cols_iota == col_of).astype(jnp.bfloat16)
        total = jnp.zeros((levels, block), jnp.float32)
        for row in range(rows):
            picked = exact_dot(values_ref[:, row, :], onehot)
            total = total + jnp.where(row_of == row, picked, 0.0)
        out_ref[...] = total

    return pl.pallas_call(
        body,
        grid=(count // block,),
        in_specs=[
            pl.BlockSpec((levels, rows, cols), lambda i: (0, 0, 0)),
            pl.BlockSpec((2, block), lambda i: (0, i)),
        ],
        out_specs=pl.BlockSpec((levels, block), lambda i: (0, i)),
        out_shape=jax.ShapeDtypeStruct((levels, count), jnp.float32),
        compiler_params=pltpu.CompilerParams(dimension_semantics=("parallel",)),
    )(values, where_to)


def add_columns(values, index_col, width, block=256):
    rows, count = values.shape

    def body(values_ref, index_ref, out_ref):
        start = pl.program_id(0) * block
        cols_iota = lax.broadcasted_iota(jnp.int32, (count, block), 1) + start
        onehot = (cols_iota == index_ref[...]).astype(jnp.bfloat16)
        out_ref[...] = exact_dot(values_ref[...], onehot)

    return pl.pallas_call(
        body,
        grid=(width // block,),
        in_specs=[
            pl.BlockSpec((rows, count), lambda i: (0, 0)),
            pl.BlockSpec((count, 1), lambda i: (0, 0)),
        ],
        out_specs=pl.BlockSpec((rows, block), lambda i: (0, i)),
        out_shape=jax.ShapeDtypeStruct((rows, width), jnp.float32),
        compiler_params=pltpu.CompilerParams(dimension_semantics=("parallel",)),
    )(values, index_col)


def all_sum(parts, axes):
    count = 1
    for axis in axes:
        count *= lax.axis_size(axis)
    flat = jnp.concatenate([part.reshape(-1) for part in parts])
    size = flat.shape[0]
    chunk = -(-size // count)
    rows = jnp.pad(flat, (0, chunk * count - size)).reshape(count, chunk)
    mine = jnp.sum(lax.all_to_all(rows, axes, 0, 0, tiled=True), axis=0)
    spread = lax.all_to_all(jnp.broadcast_to(mine[None], (count, chunk)), axes, 0, 0, tiled=True)
    flat = spread.reshape(-1)
    sums, offset = [], 0
    for part in parts:
        sums.append(flat[offset : offset + part.size].reshape(part.shape))
        offset += part.size
    return tuple(sums)


def inside_rows(tile_rows, border):
    first_row = lax.axis_index("lat") * tile_rows
    global_rows = first_row + jnp.arange(-border, tile_rows + border, dtype=jnp.int32)
    row_limit = tile_rows * lax.axis_size("lat")
    return ((global_rows >= 0) & (global_rows < row_limit)).astype(jnp.float32)[None, :, None]


def on_device(state, land_mask, observations, profile_cells, profile_counts, w_in, w_out):
    levels, tile_rows, tile_cols = state.shape
    ocean = land_mask.astype(jnp.float32)
    back_in = flipped(w_in)
    back_out = flipped(w_out)
    current = state
    history = []
    both = extended_2(
        jnp.concatenate([current, ocean[None]], axis=0), (("lon", 2), ("lat", 1)), 8
    ) * inside_rows(tile_rows, 8)
    wide, ocean_wide = both[:levels], both[levels]
    coarse_wide = wide.astype(jnp.bfloat16)
    activity_wide = jnp.tanh(conv_valid(coarse_wide, w_in))
    hidden_wide = (activity_wide * inside_rows(tile_rows, 6)).astype(jnp.bfloat16)
    closure_wide = conv_valid(hidden_wide, w_out)
    history.append(
        (coarse_wide[:, 6:-6, 6:-6], activity_wide[:, 4:-4, 4:-4], hidden_wide[:, 4:-4, 4:-4])
    )
    extended = (
        wide[:, 4:-4, 4:-4]
        + ocean_wide[None, 4:-4, 4:-4] * (diffusion * laplace(wide, 4) + closure_wide)
    ) * inside_rows(tile_rows, 4)
    current = extended[:, 4:-4, 4:-4]
    for step_index in range(1, STEPS):
        coarse = extended.astype(jnp.bfloat16)
        activity = jnp.tanh(conv_valid(coarse, w_in))
        hidden = (activity * inside_rows(tile_rows, 2)).astype(jnp.bfloat16)
        closure = conv_valid(hidden, w_out)
        history.append((coarse[:, 2:-2, 2:-2], activity, hidden))
        current = current + ocean * (diffusion * laplace(extended, 4) + closure)
    devices = lax.axis_size("lon") * lax.axis_size("lat")
    profile_dev = observations.shape[1]
    cell_count = tile_rows * tile_cols
    sent_rows = profile_counts[0]
    finish = jnp.cumsum(sent_rows)
    starts = finish - sent_rows
    slot_index = jnp.arange(CAP, dtype=jnp.int32)
    source_row = starts[:, None] + slot_index[None, :]
    filled = (slot_index[None, :] < sent_rows[:, None]).reshape(1, -1)
    picked = jnp.where(filled, source_row.reshape(1, -1), profile_dev)
    source = jnp.concatenate(
        [observations, profile_cells[None, :].astype(jnp.float32)], axis=0
    )
    source_cols = 128 if profile_dev % 128 == 0 else profile_dev
    source_rows = profile_dev // source_cols
    pick_row = (picked // source_cols)[0]
    pick_hit = pick_row[None, :] == jnp.arange(source_rows, dtype=jnp.int32)[:, None]
    pick_onehot = ((picked % source_cols)[0][None, :] == jnp.arange(source_cols)[:, None]).astype(
        jnp.bfloat16
    )
    by_source = exact_dot(source.reshape(-1, source_cols), pick_onehot)
    gathered = jnp.sum(
        jnp.where(pick_hit[None], by_source.reshape(levels + 1, source_rows, -1), 0.0), axis=1
    )
    sent_values = gathered[:levels]
    sent_cells = jnp.where(filled, gathered[levels:], float(cell_count))
    payload = jnp.concatenate([sent_values, sent_cells], axis=0)
    arrived = lax.all_to_all(payload, ("lon", "lat"), split_axis=1, concat_axis=1, tiled=True)
    received_values = arrived[:levels]
    received_cells = arrived[levels:].astype(jnp.int32)
    occupied = received_cells < cell_count
    target = jnp.where(occupied, received_cells, cell_count)
    row_of = jnp.where(occupied, received_cells // tile_cols, tile_rows)[0]
    col_of = (received_cells % tile_cols)[0]
    row_hit = row_of[None, :] == jnp.arange(tile_rows, dtype=jnp.int32)[:, None]
    col_hit = col_of[:, None] == jnp.arange(tile_cols, dtype=jnp.int32)[None, :]
    col_onehot = col_hit.astype(jnp.bfloat16)
    by_cols = exact_dot(current.reshape(levels * tile_rows, tile_cols), col_onehot.T)
    picked = jnp.sum(
        jnp.where(row_hit[None], by_cols.reshape(levels, tile_rows, -1), 0.0), axis=1
    )
    misfits = jnp.where(occupied, picked - received_values, 0.0)
    square_sum = jnp.sum(misfits * misfits)
    tangent = jnp.zeros((levels * tile_rows, tile_cols), jnp.float32)
    for part in split3(misfits / profile_dev):
        spread_rows = jnp.where(row_hit[None], part[:, None, :], jnp.zeros((), jnp.bfloat16))
        tangent = tangent + jnp.dot(
            spread_rows.reshape(levels * tile_rows, -1), col_onehot, preferred_element_type=jnp.float32
        )
    tangent = tangent.reshape(levels, tile_rows, tile_cols)
    grad_in = jnp.zeros(w_in.shape[2:] + w_in.shape[1::-1], jnp.float32)
    grad_out = jnp.zeros(w_out.shape[2:] + w_out.shape[1::-1], jnp.float32)
    for step_index in reversed(range(STEPS)):
        coarse, activity, hidden = history[step_index]
        forcing = ocean * tangent
        forcing_low = forcing.astype(jnp.bfloat16)
        grad_out = grad_out + kernel_grad(hidden, forcing_low)
        derivative = 1.0 - activity * activity
        beside_all = extended_2(forcing, (("lon", 2), ("lat", 1)), 4) * inside_rows(tile_rows, 4)
        spread = conv_valid(beside_all.astype(jnp.bfloat16), back_out)
        margin = (spread * derivative * inside_rows(tile_rows, 2)).astype(jnp.bfloat16)
        sensitivity = margin[:, 2:-2, 2:-2]
        grad_in = grad_in + kernel_grad(coarse, sensitivity)
        tangent = tangent + diffusion * laplace(beside_all, 4) + conv_valid(margin, back_in)
    grad_in, grad_out, square_sum = all_sum((grad_in, grad_out, square_sum), ("lon", "lat"))
    grad_in = jnp.transpose(grad_in, (3, 2, 0, 1))
    grad_out = jnp.transpose(grad_out, (3, 2, 0, 1))
    misfit = square_sum / (2.0 * profile_dev * devices * levels)
    return (current, misfit, grad_in, grad_out, tangent * profile_dev)


def solution(mesh):
    placed = (
        P(None, "lat", "lon"),
        P("lat", "lon"),
        P(None, ("lon", "lat")),
        P(("lon", "lat")),
        P(("lon", "lat"), None),
        P(),
        P(),
    )
    return jax.shard_map(
        on_device,
        mesh=mesh,
        in_specs=placed,
        out_specs=(P(None, "lat", "lon"), P(), P(), P(), P(None, "lat", "lon")),
        check_vma=False,
    )
```

```python
import jax
import jax.numpy as jnp
from jax import lax
from jax.experimental import pallas as pl
from jax.experimental.pallas import tpu as pltpu
from jax.sharding import PartitionSpec as P

STEPS = 2
CAP = 32


diffusion = 0.2


def extended_2(cells, sides, width):
    for axis, dim in sides:
        count = lax.axis_size(axis)
        head = lax.slice_in_dim(cells, 0, width, axis=dim)
        tail = lax.slice_in_dim(cells, cells.shape[dim] - width, cells.shape[dim], axis=dim)
        cells = jnp.concatenate(
            [
                lax.ppermute(tail, axis, [(i, (i + 1) % count) for i in range(count)]),
                cells,
                lax.ppermute(head, axis, [((i + 1) % count, i) for i in range(count)]),
            ],
            axis=dim,
        )
    return cells


def laplace(extended, border):
    height = extended.shape[1] - 2 * border
    breadth = extended.shape[2] - 2 * border

    def neighbour(offset_y, offset_x):
        return extended[
            :,
            border + offset_y : border + offset_y + height,
            border + offset_x : border + offset_x + breadth,
        ]

    return (
        neighbour(-1, 0)
        + neighbour(1, 0)
        + neighbour(0, -1)
        + neighbour(0, 1)
        - 4.0 * neighbour(0, 0)
    )


def conv_valid(padded, kernel):
    return lax.conv_general_dilated(
        padded[None],
        kernel,
        (1, 1),
        "VALID",
        dimension_numbers=("NCHW", "OIHW", "NCHW"),
        preferred_element_type=jnp.float32,
    )[0]


def flipped(kernel):
    return jnp.transpose(kernel[:, :, ::-1, ::-1], (1, 0, 2, 3))


def kernel_grad(padded, cotangent):
    return lax.conv_general_dilated(
        padded,
        cotangent,
        (1, 1),
        "VALID",
        dimension_numbers=("CNHW", "IOHW", "HWNC"),
        preferred_element_type=jnp.float32,
    )


def split3(values):
    high = lax.reduce_precision(values, exponent_bits=8, mantissa_bits=7)
    rest = values - high
    middle = lax.reduce_precision(rest, exponent_bits=8, mantissa_bits=7)
    low = rest - middle
    return high.astype(jnp.bfloat16), middle.astype(jnp.bfloat16), low.astype(jnp.bfloat16)


def exact_dot(values, onehot):
    high, middle, low = split3(values)
    dims = (((1,), (0,)), ((), ()))
    total = lax.dot_general(high, onehot, dims, preferred_element_type=jnp.float32)
    total = total + lax.dot_general(middle, onehot, dims, preferred_element_type=jnp.float32)
    return total + lax.dot_general(low, onehot, dims, preferred_element_type=jnp.float32)


def pick_columns(values, index, block=512):
    rows, width = values.shape
    count = index.shape[1]

    def body(values_ref, index_ref, out_ref):
        rows_iota = lax.broadcasted_iota(jnp.int32, (width, block), 0)
        onehot = (rows_iota == index_ref[...]).astype(jnp.bfloat16)
        out_ref[...] = exact_dot(values_ref[...], onehot)

    return pl.pallas_call(
        body,
        grid=(count // block,),
        in_specs=[
            pl.BlockSpec((rows, width), lambda i: (0, 0)),
            pl.BlockSpec((1, block), lambda i: (0, i)),
        ],
        out_specs=pl.BlockSpec((rows, block), lambda i: (0, i)),
        out_shape=jax.ShapeDtypeStruct((rows, count), jnp.float32),
        compiler_params=pltpu.CompilerParams(dimension_semantics=("parallel",)),
    )(values, index)


def pick_cells(values, where_to, block=512):
    levels, rows, cols = values.shape
    count = where_to.shape[1]

    def body(values_ref, where_ref, out_ref):
        row_of = where_ref[0:1, :]
        col_of = where_ref[1:2, :]
        cols_iota = lax.broadcasted_iota(jnp.int32, (cols, block), 0)
        onehot = (cols_iota == col_of).astype(jnp.bfloat16)
        total = jnp.zeros((levels, block), jnp.float32)
        for row in range(rows):
            picked = exact_dot(values_ref[:, row, :], onehot)
            total = total + jnp.where(row_of == row, picked, 0.0)
        out_ref[...] = total

    return pl.pallas_call(
        body,
        grid=(count // block,),
        in_specs=[
            pl.BlockSpec((levels, rows, cols), lambda i: (0, 0, 0)),
            pl.BlockSpec((2, block), lambda i: (0, i)),
        ],
        out_specs=pl.BlockSpec((levels, block), lambda i: (0, i)),
        out_shape=jax.ShapeDtypeStruct((levels, count), jnp.float32),
        compiler_params=pltpu.CompilerParams(dimension_semantics=("parallel",)),
    )(values, where_to)


def add_columns(values, index_col, width, block=256):
    rows, count = values.shape

    def body(values_ref, index_ref, out_ref):
        start = pl.program_id(0) * block
        cols_iota = lax.broadcasted_iota(jnp.int32, (count, block), 1) + start
        onehot = (cols_iota == index_ref[...]).astype(jnp.bfloat16)
        out_ref[...] = exact_dot(values_ref[...], onehot)

    return pl.pallas_call(
        body,
        grid=(width // block,),
        in_specs=[
            pl.BlockSpec((rows, count), lambda i: (0, 0)),
            pl.BlockSpec((count, 1), lambda i: (0, 0)),
        ],
        out_specs=pl.BlockSpec((rows, block), lambda i: (0, i)),
        out_shape=jax.ShapeDtypeStruct((rows, width), jnp.float32),
        compiler_params=pltpu.CompilerParams(dimension_semantics=("parallel",)),
    )(values, index_col)


def all_sum(parts, axes):
    count = 1
    for axis in axes:
        count *= lax.axis_size(axis)
    flat = jnp.concatenate([part.reshape(-1) for part in parts])
    size = flat.shape[0]
    chunk = -(-size // count)
    rows = jnp.pad(flat, (0, chunk * count - size)).reshape(count, chunk)
    mine = jnp.sum(lax.all_to_all(rows, axes, 0, 0, tiled=True), axis=0)
    spread = lax.all_to_all(jnp.broadcast_to(mine[None], (count, chunk)), axes, 0, 0, tiled=True)
    flat = spread.reshape(-1)
    sums, offset = [], 0
    for part in parts:
        sums.append(flat[offset : offset + part.size].reshape(part.shape))
        offset += part.size
    return tuple(sums)


def inside_rows(tile_rows, border):
    first_row = lax.axis_index("lat") * tile_rows
    global_rows = first_row + jnp.arange(-border, tile_rows + border, dtype=jnp.int32)
    row_limit = tile_rows * lax.axis_size("lat")
    return ((global_rows >= 0) & (global_rows < row_limit)).astype(jnp.float32)[None, :, None]


def on_device(state, land_mask, observations, profile_cells, profile_counts, w_in, w_out):
    levels, tile_rows, tile_cols = state.shape
    ocean = land_mask.astype(jnp.float32)
    back_in = flipped(w_in)
    back_out = flipped(w_out)
    current = state
    history = []
    both = extended_2(
        jnp.concatenate([current, ocean[None]], axis=0), (("lon", 2), ("lat", 1)), 8
    ) * inside_rows(tile_rows, 8)
    wide, ocean_wide = both[:levels], both[levels]
    coarse_wide = wide.astype(jnp.bfloat16)
    activity_wide = jnp.tanh(conv_valid(coarse_wide, w_in))
    hidden_wide = (activity_wide * inside_rows(tile_rows, 6)).astype(jnp.bfloat16)
    closure_wide = conv_valid(hidden_wide, w_out)
    history.append(
        (coarse_wide[:, 6:-6, 6:-6], activity_wide[:, 4:-4, 4:-4], hidden_wide[:, 4:-4, 4:-4])
    )
    extended = (
        wide[:, 4:-4, 4:-4]
        + ocean_wide[None, 4:-4, 4:-4] * (diffusion * laplace(wide, 4) + closure_wide)
    ) * inside_rows(tile_rows, 4)
    current = extended[:, 4:-4, 4:-4]
    for step_index in range(1, STEPS):
        coarse = extended.astype(jnp.bfloat16)
        activity = jnp.tanh(conv_valid(coarse, w_in))
        hidden = (activity * inside_rows(tile_rows, 2)).astype(jnp.bfloat16)
        closure = conv_valid(hidden, w_out)
        history.append((coarse[:, 2:-2, 2:-2], activity, hidden))
        current = current + ocean * (diffusion * laplace(extended, 4) + closure)
    devices = lax.axis_size("lon") * lax.axis_size("lat")
    profile_dev = observations.shape[1]
    cell_count = tile_rows * tile_cols
    sent_rows = profile_counts[0]
    finish = jnp.cumsum(sent_rows)
    starts = finish - sent_rows
    slot_index = jnp.arange(CAP, dtype=jnp.int32)
    source_row = starts[:, None] + slot_index[None, :]
    filled = (slot_index[None, :] < sent_rows[:, None]).reshape(1, -1)
    picked = jnp.where(filled, source_row.reshape(1, -1), profile_dev)
    source = jnp.concatenate(
        [observations, profile_cells[None, :].astype(jnp.float32)], axis=0
    )
    source_cols = 128 if profile_dev % 128 == 0 else profile_dev
    source_rows = profile_dev // source_cols
    pick_row = (picked // source_cols)[0]
    pick_hit = pick_row[None, :] == jnp.arange(source_rows, dtype=jnp.int32)[:, None]
    pick_onehot = ((picked % source_cols)[0][None, :] == jnp.arange(source_cols)[:, None]).astype(
        jnp.bfloat16
    )
    by_source = exact_dot(source.reshape(-1, source_cols), pick_onehot)
    gathered = jnp.sum(
        jnp.where(pick_hit[None], by_source.reshape(levels + 1, source_rows, -1), 0.0), axis=1
    )
    sent_values = gathered[:levels]
    sent_cells = jnp.where(filled, gathered[levels:], float(cell_count))
    payload = jnp.concatenate([sent_values, sent_cells], axis=0)
    arrived = lax.all_to_all(payload, ("lon", "lat"), split_axis=1, concat_axis=1, tiled=True)
    received_values = arrived[:levels]
    received_cells = arrived[levels:].astype(jnp.int32)
    occupied = received_cells < cell_count
    target = jnp.where(occupied, received_cells, cell_count)
    row_of = jnp.where(occupied, received_cells // tile_cols, tile_rows)[0]
    col_of = (received_cells % tile_cols)[0]
    row_hit = row_of[None, :] == jnp.arange(tile_rows, dtype=jnp.int32)[:, None]
    col_hit = col_of[:, None] == jnp.arange(tile_cols, dtype=jnp.int32)[None, :]
    col_onehot = col_hit.astype(jnp.bfloat16)
    by_cols = exact_dot(current.reshape(levels * tile_rows, tile_cols), col_onehot.T)
    picked = jnp.sum(
        jnp.where(row_hit[None], by_cols.reshape(levels, tile_rows, -1), 0.0), axis=1
    )
    misfits = jnp.where(occupied, picked - received_values, 0.0)
    square_sum = jnp.sum(misfits * misfits)
    tangent = jnp.zeros((levels * tile_rows, tile_cols), jnp.float32)
    for part in split3(misfits / profile_dev):
        spread_rows = jnp.where(row_hit[None], part[:, None, :], jnp.zeros((), jnp.bfloat16))
        tangent = tangent + jnp.dot(
            spread_rows.reshape(levels * tile_rows, -1), col_onehot, preferred_element_type=jnp.float32
        )
    tangent = tangent.reshape(levels, tile_rows, tile_cols)
    grad_in = jnp.zeros(w_in.shape[2:] + w_in.shape[1::-1], jnp.float32)
    grad_out = jnp.zeros(w_out.shape[2:] + w_out.shape[1::-1], jnp.float32)
    in_pairs, out_pairs = [], []
    for step_index in reversed(range(STEPS)):
        coarse, activity, hidden = history[step_index]
        forcing = ocean * tangent
        forcing_low = forcing.astype(jnp.bfloat16)
        out_pairs.append((hidden, forcing_low))
        derivative = 1.0 - activity * activity
        beside_all = extended_2(forcing, (("lon", 2), ("lat", 1)), 4) * inside_rows(tile_rows, 4)
        spread = conv_valid(beside_all.astype(jnp.bfloat16), back_out)
        margin = (spread * derivative * inside_rows(tile_rows, 2)).astype(jnp.bfloat16)
        sensitivity = margin[:, 2:-2, 2:-2]
        in_pairs.append((coarse, sensitivity))
        tangent = tangent + diffusion * laplace(beside_all, 4) + conv_valid(margin, back_in)
    grad_in = kernel_grad(
        jnp.stack([pair[0] for pair in in_pairs]), jnp.stack([pair[1] for pair in in_pairs])
    )
    grad_out = kernel_grad(
        jnp.stack([pair[0] for pair in out_pairs]), jnp.stack([pair[1] for pair in out_pairs])
    )
    grad_in, grad_out, square_sum = all_sum((grad_in, grad_out, square_sum), ("lon", "lat"))
    grad_in = jnp.transpose(grad_in, (3, 2, 0, 1))
    grad_out = jnp.transpose(grad_out, (3, 2, 0, 1))
    misfit = square_sum / (2.0 * profile_dev * devices * levels)
    return (current, misfit, grad_in, grad_out, tangent * profile_dev)


def solution(mesh):
    placed = (
        P(None, "lat", "lon"),
        P("lat", "lon"),
        P(None, ("lon", "lat")),
        P(("lon", "lat")),
        P(("lon", "lat"), None),
        P(),
        P(),
    )
    return jax.shard_map(
        on_device,
        mesh=mesh,
        in_specs=placed,
        out_specs=(P(None, "lat", "lon"), P(), P(), P(), P(None, "lat", "lon")),
        check_vma=False,
    )
```
